256 devices in a mesh: ctx: 16 (over z, core), ch: 16 (over y, x).
Axes of the slice: x: 4, y: 4, z: 8, core: 2. Of those that a mesh axis runs over, the one named last changes fastest.
Arguments:
- inputs: bfloat16 [4096, 4096], P('ctx', 'ch'), may hold values from -6 to 6
- gating: bfloat16 [4096, 4096], P('ctx', 'ch'), may hold values from -6 to 6
- filter_taps: bfloat16 [4096, 4096], P('ctx', 'ch'), may hold values from -2.25 to 2.25
- skip_gain: float32 [4096], P('ch'), may hold values from 0.5 to 1.5
- w_out: bfloat16 [4096, 4096], P('ch'), may hold values from -0.09375 to 0.09375
- cotangent: bfloat16 [4096, 4096], P('ctx', 'ch'), may hold values from -0.3125 to 0.3125
Outputs:
- output: bfloat16 [4096, 4096], P('ctx', 'ch')
- filter_grad: float32 [4096, 4096], P('ctx', 'ch')
The draws below stay inside these ranges and needn't reach their ends.
All inputs are finite; a program needn't handle non-finite values.
Results may differ from the reference program's by a relative error of at most 0.015.
Values may be sent and summed in bfloat16 or wider, within the bound.
No kernel may reach another device: no remote copies, remote signals or barrier semaphores. Data moves between devices by JAX's collectives and lax.ppermute only.
A program may use at most 64 MiB of HBM per device.

```python
import math
import jax
import jax.numpy as jnp

D = 4096
TOKEN_COUNT = 4096


def draw_filter_taps(key, part):
    random_key_split = jax.random.split(key, 7)
    delay_offsets = jnp.arange(TOKEN_COUNT, dtype=jnp.float32)[:, None]
    slow_share = 0.5
    noisy_component = jnp.clip(jax.random.normal(random_key_split[0], (TOKEN_COUNT, D), jnp.float32), -5.0, 5.0)
    chooser = jax.random.uniform(random_key_split[1], (1, D), jnp.float32)
    slow_len = jnp.exp(jax.random.uniform(random_key_split[2], (1, D), jnp.float32, math.log(TOKEN_COUNT * 0.5), math.log(TOKEN_COUNT * 8.0)))
    quick_len = jnp.exp(jax.random.uniform(random_key_split[3], (1, D), jnp.float32, math.log(10.0), math.log(60.0)))
    decay_length = jnp.where(chooser < slow_share, slow_len, quick_len)
    spike_positions = jax.random.randint(random_key_split[4], (3,), 1, TOKEN_COUNT).astype(jnp.float32)
    spike_keep_mask = jax.random.uniform(random_key_split[6], (3,), jnp.float32, 0.5, 0.8)
    spike_envelope = jnp.prod(jnp.where(delay_offsets >= spike_positions[None, :], spike_keep_mask[None, :], 1.0), axis=1, keepdims=True)
    filter_power = 0.5 * decay_length * (1.0 - jnp.exp(-2.0 * TOKEN_COUNT / decay_length))
    sampled_filter = noisy_component * jnp.exp(-delay_offsets / decay_length) * spike_envelope / jnp.sqrt(filter_power)
    return sampled_filter.astype(jnp.bfloat16)


def steps_of(own_key, shape, cuts, smallest, high):
    level = 1.0
    for dim, blocks in cuts:
        draws = jax.random.uniform(jax.random.fold_in(jax.random.fold_in(own_key, 6), dim), (blocks,), jnp.float32, smallest / len(cuts), high / len(cuts))
        level = level * jnp.repeat(jnp.exp(draws), shape[dim] // blocks).reshape((-1,) + (1,) * (len(shape) - 1 - dim))
    return level


def scatter_about(own_key, shape, width, most, shards=(), kind=jnp.bfloat16):
    drawn = jax.random.normal(own_key, shape, jnp.float32) * width
    if len(shards) > 0:
        drawn = steps_of(own_key, shape, shards, -0.22, 0.18) * drawn
    return jnp.clip(drawn, min=-most, max=most).astype(kind)


def setup_inputs(seed: int = 0) -> dict:
    arg_keys = jax.random.split(jax.random.key(seed), 7)
    return {
        "inputs": scatter_about(arg_keys[0], (TOKEN_COUNT, D), 1.0, 6.0, ((0, 16), (1, 16))),
        "gating": scatter_about(arg_keys[1], (TOKEN_COUNT, D), 1.0, 6.0, ((0, 16), (1, 16))),
        "filter_taps": draw_filter_taps(jax.random.fold_in(arg_keys[6], 71), 0),
        "skip_gain": jnp.clip(0.5 + 1.0 * jax.random.uniform(arg_keys[3], (D,), jnp.float32) ** steps_of(arg_keys[3], (D,), ((0, 16),), -0.2, 0.2), 0.5, 1.5),
        "w_out": scatter_about(arg_keys[4], (D, D), D ** -0.5, 0.09375, ((0, 16),)),
        "cotangent": scatter_about(arg_keys[5], (TOKEN_COUNT, D), 0.02, 0.3125, ((0, 16), (1, 16))),
    }


def causal_conv(signal, kernel):
    length = signal.shape[0]
    padded = 2 * length
    spectrum = jnp.fft.rfft(signal, n=padded, axis=0) * jnp.fft.rfft(kernel, n=padded, axis=0)
    return jnp.fft.irfft(spectrum, n=padded, axis=0)[:length].astype(signal.dtype)


def lagged_corr(later_rows, earlier):
    length = later_rows.shape[0]
    padded = 2 * length
    spectrum = jnp.fft.rfft(later_rows, n=padded, axis=0) * jnp.conj(jnp.fft.rfft(earlier, n=padded, axis=0))
    return jnp.fft.irfft(spectrum, n=padded, axis=0)[:length].astype(later_rows.dtype)


def reference(inputs, gating, filter_taps, skip_gain, w_out, cotangent):
    signal = inputs.astype(jnp.float32)
    gate_wide = gating.astype(jnp.float32)
    convolved = causal_conv(signal, filter_taps.astype(jnp.float32))
    mixed_sum = convolved + skip_gain[None, :] * signal
    gated_rows = (gate_wide * mixed_sum).astype(jnp.bfloat16)
    output = jnp.dot(gated_rows, w_out, preferred_element_type=jnp.float32).astype(jnp.bfloat16)
    upstream = jnp.dot(cotangent, w_out.T, preferred_element_type=jnp.float32)
    grad_mixed = upstream * gate_wide
    filter_grad = lagged_corr(grad_mixed, signal)
    return output, filter_grad
```

```python
import math

import jax
import jax.numpy as jnp
from jax import lax
from jax.sharding import PartitionSpec as P

exact_prec = lax.Precision.HIGHEST


def spectral_tables(block_len):
    time_ids = jnp.arange(2 * block_len, dtype=jnp.int32)
    freq_ids = jnp.arange(block_len, dtype=jnp.int32)
    phase_ids = freq_ids[:, None] * time_ids[None, :] % (2 * block_len)
    angles = phase_ids.astype(jnp.float32) * (math.pi / block_len)
    parity = jnp.where(time_ids % 2 == 0, 1.0, -1.0).astype(jnp.float32)[None, :]
    is_first = (freq_ids == 0)[:, None]
    forward = jnp.concatenate(
        [jnp.cos(angles), jnp.where(is_first, parity, -jnp.sin(angles))], axis=0
    )
    norm_scale = 1.0 / (2 * block_len)
    real_rows = jnp.where(is_first, 1.0, 2.0) * jnp.cos(angles) * norm_scale
    imag_rows = jnp.where(is_first, parity, -2.0 * jnp.sin(angles)) * norm_scale
    inverse = jnp.concatenate([real_rows, imag_rows], axis=0).T
    first_bin = is_first.astype(jnp.float32)
    return (forward, inverse, first_bin)


def spec_product(first_spec, second_spec, first_bin):
    bin_count = first_bin.shape[0]
    first_real, first_imag = (first_spec[..., :bin_count, :], first_spec[..., bin_count:, :])
    second_real, second_imag = (second_spec[..., :bin_count, :], second_spec[..., bin_count:, :])
    others = 1.0 - first_bin
    real_part = first_real * second_real - others * first_imag * second_imag
    imag_part = (
        others * (first_real * second_imag + first_imag * second_real)
        + first_bin * first_imag * second_imag
    )
    return jnp.concatenate([real_part, imag_part], axis=-2)


def conj_product(first_spec, second_spec, first_bin):
    bin_count = first_bin.shape[0]
    first_real, first_imag = (first_spec[..., :bin_count, :], first_spec[..., bin_count:, :])
    second_real, second_imag = (second_spec[..., :bin_count, :], second_spec[..., bin_count:, :])
    others = 1.0 - first_bin
    real_part = first_real * second_real + others * first_imag * second_imag
    imag_part = (
        others * (first_imag * second_real - first_real * second_imag)
        + first_bin * first_imag * second_imag
    )
    return jnp.concatenate([real_part, imag_part], axis=-2)


def transform(dft_table, block_rows):
    return jnp.dot(dft_table, block_rows.astype(jnp.float32), precision=exact_prec)


def shift_blocks(spec, blocks, width):
    if blocks == 0:
        return spec
    rows = spec.shape[0]
    pad = jnp.zeros((rows, blocks * width), spec.dtype)
    return jnp.concatenate([pad, spec[:, : spec.shape[1] - blocks * width]], axis=1)


def body(inputs, gating, filter_taps, skip_gain, w_out, cotangent):
    block_len, channels = inputs.shape
    ctx_count = lax.axis_size("ctx")
    width = channels // ctx_count
    forward, inverse, first_bin = spectral_tables(block_len)
    first_half = forward[:, :block_len]
    second_half = forward[:, block_len:]

    pair = jnp.stack([inputs, filter_taps])
    pair_t = lax.all_to_all(pair, "ctx", 2, 2, tiled=True)
    signal_t, taps_t = pair_t[0], pair_t[1]

    upstream = lax.dot_general(
        lax.all_gather(cotangent, "ch", axis=1, tiled=True),
        w_out,
        (((1,), (1,)), ((), ())),
        preferred_element_type=jnp.float32,
    )
    gate_wide = gating.astype(jnp.float32)
    grad_mixed = upstream * gate_wide
    grad_t = lax.all_to_all(grad_mixed, "ctx", 1, 1, tiled=True)

    low_spec = transform(first_half, signal_t)
    high_spec = transform(second_half, signal_t)
    seg_spec = high_spec + shift_blocks(low_spec, 1, width)
    taps_spec = transform(first_half, taps_t)
    grad_spec = transform(second_half, grad_t)

    running = jnp.zeros_like(seg_spec)
    lag_terms = []
    for lag in range(ctx_count):
        shifted = shift_blocks(seg_spec, lag, width)
        tap_block = taps_spec[:, lag * width : (lag + 1) * width]
        running = running + spec_product(
            jnp.tile(tap_block, (1, ctx_count)), shifted, first_bin
        )
        term = conj_product(grad_spec, shifted, first_bin)
        lag_terms.append(
            term.reshape(term.shape[0], ctx_count, width).sum(axis=1)
        )
    lag_spec = jnp.concatenate(lag_terms, axis=1)

    convolved_t = jnp.dot(inverse[block_len:], running, precision=exact_prec)
    filter_grad_t = jnp.dot(inverse[:block_len], lag_spec, precision=exact_prec)
    back = lax.all_to_all(
        jnp.stack([convolved_t, filter_grad_t]), "ctx", 2, 2, tiled=True
    )
    convolved, filter_grad = back[0], back[1]

    mixed_sum = convolved + skip_gain[None, :] * inputs.astype(jnp.float32)
    gated_rows = (gate_wide * mixed_sum).astype(jnp.bfloat16)
    partial_out = jnp.dot(gated_rows, w_out, preferred_element_type=jnp.float32)
    output = lax.psum_scatter(
        partial_out.astype(jnp.bfloat16), "ch", scatter_dimension=1, tiled=True
    )
    return (output, filter_grad)


def solution(mesh):
    return jax.shard_map(
        body,
        mesh=mesh,
        in_specs=(
            P("ctx", "ch"),
            P("ctx", "ch"),
            P("ctx", "ch"),
            P("ch"),
            P("ch", None),
            P("ctx", "ch"),
        ),
        out_specs=(P("ctx", "ch"), P("ctx", "ch")),
        check_vma=False,
    )
```

```python
import math

import jax
import jax.numpy as jnp
from jax import lax
from jax.sharding import PartitionSpec as P

exact_prec = lax.Precision.HIGHEST


def spectral_tables(block_len):
    time_ids = jnp.arange(2 * block_len, dtype=jnp.int32)
    freq_ids = jnp.arange(block_len, dtype=jnp.int32)
    phase_ids = freq_ids[:, None] * time_ids[None, :] % (2 * block_len)
    angles = phase_ids.astype(jnp.float32) * (math.pi / block_len)
    parity = jnp.where(time_ids % 2 == 0, 1.0, -1.0).astype(jnp.float32)[None, :]
    is_first = (freq_ids == 0)[:, None]
    forward = jnp.concatenate(
        [jnp.cos(angles), jnp.where(is_first, parity, -jnp.sin(angles))], axis=0
    )
    norm_scale = 1.0 / (2 * block_len)
    real_rows = jnp.where(is_first, 1.0, 2.0) * jnp.cos(angles) * norm_scale
    imag_rows = jnp.where(is_first, parity, -2.0 * jnp.sin(angles)) * norm_scale
    inverse = jnp.concatenate([real_rows, imag_rows], axis=0).T
    first_bin = is_first.astype(jnp.float32)
    return (forward, inverse, first_bin)


def spec_product(first_spec, second_spec, first_bin):
    bin_count = first_bin.shape[0]
    first_real, first_imag = (first_spec[..., :bin_count, :], first_spec[..., bin_count:, :])
    second_real, second_imag = (second_spec[..., :bin_count, :], second_spec[..., bin_count:, :])
    others = 1.0 - first_bin
    real_part = first_real * second_real - others * first_imag * second_imag
    imag_part = (
        others * (first_real * second_imag + first_imag * second_real)
        + first_bin * first_imag * second_imag
    )
    return jnp.concatenate([real_part, imag_part], axis=-2)


def conj_product(first_spec, second_spec, first_bin):
    bin_count = first_bin.shape[0]
    first_real, first_imag = (first_spec[..., :bin_count, :], first_spec[..., bin_count:, :])
    second_real, second_imag = (second_spec[..., :bin_count, :], second_spec[..., bin_count:, :])
    others = 1.0 - first_bin
    real_part = first_real * second_real + others * first_imag * second_imag
    imag_part = (
        others * (first_imag * second_real - first_real * second_imag)
        + first_bin * first_imag * second_imag
    )
    return jnp.concatenate([real_part, imag_part], axis=-2)


def transform(dft_table, block_rows):
    return jnp.dot(dft_table, block_rows.astype(jnp.float32), precision=exact_prec)


def shift_blocks(spec, blocks, width):
    if blocks == 0:
        return spec
    rows = spec.shape[0]
    pad = jnp.zeros((rows, blocks * width), spec.dtype)
    return jnp.concatenate([pad, spec[:, : spec.shape[1] - blocks * width]], axis=1)


def body(inputs, gating, filter_taps, skip_gain, w_out, cotangent):
    block_len, channels = inputs.shape
    ctx_count = lax.axis_size("ctx")
    width = channels // ctx_count
    forward, inverse, first_bin = spectral_tables(block_len)
    first_half = forward[:, :block_len]
    second_half = forward[:, block_len:]

    pair = jnp.stack([inputs, filter_taps])
    pair_t = lax.all_to_all(pair, "ctx", 2, 2, tiled=True)
    signal_t, taps_t = pair_t[0], pair_t[1]

    ch_count = lax.axis_size("ch")
    cot_rows = lax.all_to_all(
        jnp.tile(cotangent, (1, ch_count)), "ch", 1, 1, tiled=True
    )
    upstream = lax.dot_general(
        cot_rows,
        w_out,
        (((1,), (1,)), ((), ())),
        preferred_element_type=jnp.float32,
    )
    gate_wide = gating.astype(jnp.float32)
    grad_mixed = upstream * gate_wide
    grad_t = lax.all_to_all(grad_mixed, "ctx", 1, 1, tiled=True)

    low_spec = transform(first_half, signal_t)
    high_spec = transform(second_half, signal_t)
    seg_spec = high_spec + shift_blocks(low_spec, 1, width)
    taps_spec = transform(first_half, taps_t)
    grad_spec = transform(second_half, grad_t)

    running = jnp.zeros_like(seg_spec)
    lag_terms = []
    for lag in range(ctx_count):
        shifted = shift_blocks(seg_spec, lag, width)
        tap_block = taps_spec[:, lag * width : (lag + 1) * width]
        running = running + spec_product(
            jnp.tile(tap_block, (1, ctx_count)), shifted, first_bin
        )
        term = conj_product(grad_spec, shifted, first_bin)
        lag_terms.append(
            term.reshape(term.shape[0], ctx_count, width).sum(axis=1)
        )
    lag_spec = jnp.concatenate(lag_terms, axis=1)

    convolved_t = jnp.dot(inverse[block_len:], running, precision=exact_prec)
    convolved = lax.all_to_all(convolved_t, "ctx", 1, 1, tiled=True)

    mixed_sum = convolved + skip_gain[None, :] * inputs.astype(jnp.float32)
    gated_rows = (gate_wide * mixed_sum).astype(jnp.bfloat16)
    partial_out = jnp.dot(gated_rows, w_out, preferred_element_type=jnp.float32)
    pieces = lax.all_to_all(partial_out.astype(jnp.bfloat16), "ch", 1, 0, tiled=True)

    filter_grad_t = jnp.dot(inverse[:block_len], lag_spec, precision=exact_prec)
    filter_grad = lax.all_to_all(filter_grad_t, "ctx", 1, 1, tiled=True)

    output = (
        pieces.astype(jnp.float32)
        .reshape(ch_count, block_len, channels)
        .sum(axis=0)
        .astype(jnp.bfloat16)
    )
    return (output, filter_grad)


def solution(mesh):
    return jax.shard_map(
        body,
        mesh=mesh,
        in_specs=(
            P("ctx", "ch"),
            P("ctx", "ch"),
            P("ctx", "ch"),
            P("ch"),
            P("ch", None),
            P("ctx", "ch"),
        ),
        out_specs=(P("ctx", "ch"), P("ctx", "ch")),
        check_vma=False,
    )
```

```python
import functools
import math

import jax
import jax.numpy as jnp
from jax import lax
from jax.experimental import pallas as pl
from jax.experimental.pallas import tpu as pltpu
from jax.sharding import PartitionSpec as P

exact_prec = lax.Precision.HIGHEST


def spectral_tables(block_len):
    time_ids = jnp.arange(2 * block_len, dtype=jnp.int32)
    freq_ids = jnp.arange(block_len, dtype=jnp.int32)
    phase_ids = freq_ids[:, None] * time_ids[None, :] % (2 * block_len)
    angles = phase_ids.astype(jnp.float32) * (math.pi / block_len)
    parity = jnp.where(time_ids % 2 == 0, 1.0, -1.0).astype(jnp.float32)[None, :]
    is_first = (freq_ids == 0)[:, None]
    forward = jnp.concatenate(
        [jnp.cos(angles), jnp.where(is_first, parity, -jnp.sin(angles))], axis=0
    )
    norm_scale = 1.0 / (2 * block_len)
    real_rows = jnp.where(is_first, 1.0, 2.0) * jnp.cos(angles) * norm_scale
    imag_rows = jnp.where(is_first, parity, -2.0 * jnp.sin(angles)) * norm_scale
    inverse = jnp.concatenate([real_rows, imag_rows], axis=0).T
    first_bin = is_first.astype(jnp.float32)
    return (forward, inverse, first_bin)


def spec_product(first_spec, second_spec, first_bin):
    bin_count = first_bin.shape[0]
    first_real, first_imag = (first_spec[..., :bin_count, :], first_spec[..., bin_count:, :])
    second_real, second_imag = (second_spec[..., :bin_count, :], second_spec[..., bin_count:, :])
    others = 1.0 - first_bin
    real_part = first_real * second_real - others * first_imag * second_imag
    imag_part = (
        others * (first_real * second_imag + first_imag * second_real)
        + first_bin * first_imag * second_imag
    )
    return jnp.concatenate([real_part, imag_part], axis=-2)


def conj_product(first_spec, second_spec, first_bin):
    bin_count = first_bin.shape[0]
    first_real, first_imag = (first_spec[..., :bin_count, :], first_spec[..., bin_count:, :])
    second_real, second_imag = (second_spec[..., :bin_count, :], second_spec[..., bin_count:, :])
    others = 1.0 - first_bin
    real_part = first_real * second_real + others * first_imag * second_imag
    imag_part = (
        others * (first_imag * second_real - first_real * second_imag)
        + first_bin * first_imag * second_imag
    )
    return jnp.concatenate([real_part, imag_part], axis=-2)


def transform(dft_table, block_rows):
    return jnp.dot(dft_table, block_rows.astype(jnp.float32), precision=exact_prec)


def shift_blocks(spec, blocks, width):
    if blocks == 0:
        return spec
    rows = spec.shape[0]
    pad = jnp.zeros((rows, blocks * width), spec.dtype)
    return jnp.concatenate([pad, spec[:, : spec.shape[1] - blocks * width]], axis=1)


def to_slabs(spec, blocks, width):
    bins = spec.shape[0]
    slab = spec.reshape(bins, blocks, width).transpose(1, 0, 2)
    return slab.reshape(blocks, bins * width // 128, 128)


def from_slabs(slab, width):
    blocks = slab.shape[0]
    bins = slab.shape[1] * 128 // width
    spec = slab.reshape(blocks, bins, width).transpose(1, 0, 2)
    return spec.reshape(bins, blocks * width)


def block_products_kernel(width, seg_ref, taps_ref, grad_ref, conv_ref, lag_ref):
    blocks, rows, lanes = seg_ref.shape
    half = rows // 2
    row_ids = lax.broadcasted_iota(jnp.int32, (half, lanes), 0)
    lane_ids = lax.broadcasted_iota(jnp.int32, (half, lanes), 1)
    first_bin = (row_ids == 0) & (lane_ids < width)
    zero = jnp.zeros((half, lanes), jnp.float32)

    def parts(ref, i):
        return ref[i, :half, :], ref[i, half:, :]

    for p in range(blocks):
        acc_re, acc_im = zero, zero
        for k in range(p + 1):
            a_re, a_im = parts(taps_ref, k)
            b_re, b_im = parts(seg_ref, p - k)
            both_im = a_im * b_im
            acc_re = acc_re + a_re * b_re - jnp.where(first_bin, 0.0, both_im)
            acc_im = acc_im + jnp.where(first_bin, both_im, a_re * b_im + a_im * b_re)
        conv_ref[p, :half, :] = acc_re
        conv_ref[p, half:, :] = acc_im

    for k in range(blocks):
        acc_re, acc_im = zero, zero
        for p in range(k, blocks):
            a_re, a_im = parts(grad_ref, p)
            b_re, b_im = parts(seg_ref, p - k)
            both_im = a_im * b_im
            acc_re = acc_re + a_re * b_re + jnp.where(first_bin, 0.0, both_im)
            acc_im = acc_im + jnp.where(first_bin, both_im, a_im * b_re - a_re * b_im)
        lag_ref[k, :half, :] = acc_re
        lag_ref[k, half:, :] = acc_im


def block_products(seg_slab, taps_slab, grad_slab, width):
    blocks, rows, lanes = seg_slab.shape
    pairs = blocks * (blocks + 1)
    vmem = pl.BlockSpec(memory_space=pltpu.VMEM)
    shape = jax.ShapeDtypeStruct(seg_slab.shape, jnp.float32)
    return pl.pallas_call(
        functools.partial(block_products_kernel, width),
        out_shape=(shape, shape),
        in_specs=[vmem, vmem, vmem],
        out_specs=(vmem, vmem),
        cost_estimate=pl.CostEstimate(
            flops=pairs * rows * lanes * 4,
            bytes_accessed=5 * blocks * rows * lanes * 4,
            transcendentals=0,
        ),
    )(seg_slab, taps_slab, grad_slab)


def body(inputs, gating, filter_taps, skip_gain, w_out, cotangent):
    block_len, channels = inputs.shape
    ctx_count = lax.axis_size("ctx")
    width = channels // ctx_count
    forward, inverse, first_bin = spectral_tables(block_len)
    first_half = forward[:, :block_len]
    second_half = forward[:, block_len:]

    pair = jnp.stack([inputs, filter_taps])
    pair_t = lax.all_to_all(pair, "ctx", 2, 2, tiled=True)
    signal_t, taps_t = pair_t[0], pair_t[1]

    ch_count = lax.axis_size("ch")
    cot_rows = lax.all_to_all(
        jnp.tile(cotangent, (1, ch_count)), "ch", 1, 1, tiled=True
    )
    upstream = lax.dot_general(
        cot_rows,
        w_out,
        (((1,), (1,)), ((), ())),
        preferred_element_type=jnp.float32,
    )
    gate_wide = gating.astype(jnp.float32)
    grad_mixed = upstream * gate_wide
    grad_t = lax.all_to_all(grad_mixed, "ctx", 1, 1, tiled=True)

    low_spec = transform(first_half, signal_t)
    high_spec = transform(second_half, signal_t)
    seg_spec = high_spec + shift_blocks(low_spec, 1, width)
    taps_spec = transform(first_half, taps_t)
    grad_spec = transform(second_half, grad_t)

    conv_slab, lag_slab = block_products(
        to_slabs(seg_spec, ctx_count, width),
        to_slabs(taps_spec, ctx_count, width),
        to_slabs(grad_spec, ctx_count, width),
        width,
    )
    running = from_slabs(conv_slab, width)
    lag_spec = from_slabs(lag_slab, width)

    convolved_t = jnp.dot(inverse[block_len:], running, precision=exact_prec)
    convolved = lax.all_to_all(convolved_t, "ctx", 1, 1, tiled=True)

    mixed_sum = convolved + skip_gain[None, :] * inputs.astype(jnp.float32)
    gated_rows = (gate_wide * mixed_sum).astype(jnp.bfloat16)
    partial_out = jnp.dot(gated_rows, w_out, preferred_element_type=jnp.float32)
    pieces = lax.all_to_all(partial_out.astype(jnp.bfloat16), "ch", 1, 0, tiled=True)

    filter_grad_t = jnp.dot(inverse[:block_len], lag_spec, precision=exact_prec)
    filter_grad = lax.all_to_all(filter_grad_t, "ctx", 1, 1, tiled=True)

    output = (
        pieces.astype(jnp.float32)
        .reshape(ch_count, block_len, channels)
        .sum(axis=0)
        .astype(jnp.bfloat16)
    )
    return (output, filter_grad)


def solution(mesh):
    return jax.shard_map(
        body,
        mesh=mesh,
        in_specs=(
            P("ctx", "ch"),
            P("ctx", "ch"),
            P("ctx", "ch"),
            P("ch"),
            P("ch", None),
            P("ctx", "ch"),
        ),
        out_specs=(P("ctx", "ch"), P("ctx", "ch")),
        check_vma=False,
    )
```

```python
import functools
import math

import jax
import jax.numpy as jnp
from jax import lax
from jax.experimental import pallas as pl
from jax.experimental.pallas import tpu as pltpu
from jax.sharding import PartitionSpec as P

exact_prec = lax.Precision.HIGHEST


def spectral_tables(block_len):
    time_ids = jnp.arange(2 * block_len, dtype=jnp.int32)
    freq_ids = jnp.arange(block_len, dtype=jnp.int32)
    phase_ids = freq_ids[:, None] * time_ids[None, :] % (2 * block_len)
    angles = phase_ids.astype(jnp.float32) * (math.pi / block_len)
    parity = jnp.where(time_ids % 2 == 0, 1.0, -1.0).astype(jnp.float32)[None, :]
    is_first = (freq_ids == 0)[:, None]
    forward = jnp.concatenate(
        [jnp.cos(angles), jnp.where(is_first, parity, -jnp.sin(angles))], axis=0
    )
    norm_scale = 1.0 / (2 * block_len)
    real_rows = jnp.where(is_first, 1.0, 2.0) * jnp.cos(angles) * norm_scale
    imag_rows = jnp.where(is_first, parity, -2.0 * jnp.sin(angles)) * norm_scale
    inverse = jnp.concatenate([real_rows, imag_rows], axis=0).T
    first_bin = is_first.astype(jnp.float32)
    return (forward, inverse, first_bin)


def spec_product(first_spec, second_spec, first_bin):
    bin_count = first_bin.shape[0]
    first_real, first_imag = (first_spec[..., :bin_count, :], first_spec[..., bin_count:, :])
    second_real, second_imag = (second_spec[..., :bin_count, :], second_spec[..., bin_count:, :])
    others = 1.0 - first_bin
    real_part = first_real * second_real - others * first_imag * second_imag
    imag_part = (
        others * (first_real * second_imag + first_imag * second_real)
        + first_bin * first_imag * second_imag
    )
    return jnp.concatenate([real_part, imag_part], axis=-2)


def conj_product(first_spec, second_spec, first_bin):
    bin_count = first_bin.shape[0]
    first_real, first_imag = (first_spec[..., :bin_count, :], first_spec[..., bin_count:, :])
    second_real, second_imag = (second_spec[..., :bin_count, :], second_spec[..., bin_count:, :])
    others = 1.0 - first_bin
    real_part = first_real * second_real + others * first_imag * second_imag
    imag_part = (
        others * (first_imag * second_real - first_real * second_imag)
        + first_bin * first_imag * second_imag
    )
    return jnp.concatenate([real_part, imag_part], axis=-2)


def transform(dft_table, block_rows):
    return jnp.dot(dft_table, block_rows.astype(jnp.float32), precision=exact_prec)


def shift_blocks(spec, blocks, width):
    if blocks == 0:
        return spec
    rows = spec.shape[0]
    pad = jnp.zeros((rows, blocks * width), spec.dtype)
    return jnp.concatenate([pad, spec[:, : spec.shape[1] - blocks * width]], axis=1)


def block_products_kernel(width, low_ref, high_ref, taps_ref, grad_ref, conv_ref, lag_ref, seg_ref):
    rows, bins = low_ref.shape
    blocks = rows // width
    half = bins // 2
    for p in range(blocks):
        here = pl.ds(p * width, width)
        if p == 0:
            seg_ref[here, :] = high_ref[here, :]
        else:
            seg_ref[here, :] = high_ref[here, :] + low_ref[pl.ds((p - 1) * width, width), :]
    lane_ids = lax.broadcasted_iota(jnp.int32, (width, half), 1)
    first_bin = lane_ids == 0
    zero = jnp.zeros((width, half), jnp.float32)

    def parts(ref, i):
        rows_i = pl.ds(i * width, width)
        return ref[rows_i, :half], ref[rows_i, half:]

    for p in range(blocks):
        acc_re, acc_im = zero, zero
        for k in range(p + 1):
            a_re, a_im = parts(taps_ref, k)
            b_re, b_im = parts(seg_ref, p - k)
            both_im = a_im * b_im
            acc_re = acc_re + a_re * b_re - jnp.where(first_bin, 0.0, both_im)
            acc_im = acc_im + jnp.where(first_bin, both_im, a_re * b_im + a_im * b_re)
        conv_ref[pl.ds(p * width, width), :half] = acc_re
        conv_ref[pl.ds(p * width, width), half:] = acc_im

    for k in range(blocks):
        acc_re, acc_im = zero, zero
        for p in range(k, blocks):
            a_re, a_im = parts(grad_ref, p)
            b_re, b_im = parts(seg_ref, p - k)
            both_im = a_im * b_im
            acc_re = acc_re + a_re * b_re + jnp.where(first_bin, 0.0, both_im)
            acc_im = acc_im + jnp.where(first_bin, both_im, a_im * b_re - a_re * b_im)
        lag_ref[pl.ds(k * width, width), :half] = acc_re
        lag_ref[pl.ds(k * width, width), half:] = acc_im


def block_products(low_spec, high_spec, taps_spec, grad_spec, width):
    rows, bins = low_spec.shape
    blocks = rows // width
    pairs = blocks * (blocks + 1)
    vmem = pl.BlockSpec(memory_space=pltpu.VMEM)
    shape = jax.ShapeDtypeStruct(low_spec.shape, jnp.float32)
    return pl.pallas_call(
        functools.partial(block_products_kernel, width),
        out_shape=(shape, shape),
        in_specs=[vmem, vmem, vmem, vmem],
        out_specs=(vmem, vmem),
        scratch_shapes=[pltpu.VMEM(low_spec.shape, jnp.float32)],
        cost_estimate=pl.CostEstimate(
            flops=pairs * width * bins * 4,
            bytes_accessed=6 * rows * bins * 4,
            transcendentals=0,
        ),
    )(low_spec, high_spec, taps_spec, grad_spec)


def transform_t(dft_table, block_rows):
    return lax.dot_general(
        block_rows.astype(jnp.float32), dft_table, (((0,), (1,)), ((), ())),
        precision=exact_prec,
    )


def inverse_t(inverse_rows, spec_t):
    return lax.dot_general(
        inverse_rows, spec_t, (((1,), (1,)), ((), ())), precision=exact_prec
    )


def body(inputs, gating, filter_taps, skip_gain, w_out, cotangent):
    block_len, channels = inputs.shape
    ctx_count = lax.axis_size("ctx")
    width = channels // ctx_count
    forward, inverse, first_bin = spectral_tables(block_len)
    first_half = forward[:, :block_len]
    second_half = forward[:, block_len:]

    pair = jnp.stack([inputs, filter_taps])
    pair_t = lax.all_to_all(pair, "ctx", 2, 2, tiled=True)
    signal_t, taps_t = pair_t[0], pair_t[1]

    ch_count = lax.axis_size("ch")
    cot_rows = lax.all_to_all(
        jnp.tile(cotangent, (1, ch_count)), "ch", 1, 1, tiled=True
    )
    upstream = lax.dot_general(
        cot_rows,
        w_out,
        (((1,), (1,)), ((), ())),
        preferred_element_type=jnp.float32,
    )
    gate_wide = gating.astype(jnp.float32)
    grad_mixed = upstream * gate_wide
    grad_t = lax.all_to_all(grad_mixed, "ctx", 1, 1, tiled=True)

    conv_spec, lag_spec = block_products(
        transform_t(first_half, signal_t),
        transform_t(second_half, signal_t),
        transform_t(first_half, taps_t),
        transform_t(second_half, grad_t),
        width,
    )

    convolved_t = inverse_t(inverse[block_len:], conv_spec)
    convolved = lax.all_to_all(convolved_t, "ctx", 1, 1, tiled=True)

    mixed_sum = convolved + skip_gain[None, :] * inputs.astype(jnp.float32)
    gated_rows = (gate_wide * mixed_sum).astype(jnp.bfloat16)
    partial_out = jnp.dot(gated_rows, w_out, preferred_element_type=jnp.float32)
    pieces = lax.all_to_all(partial_out.astype(jnp.bfloat16), "ch", 1, 0, tiled=True)

    filter_grad_t = inverse_t(inverse[:block_len], lag_spec)
    filter_grad = lax.all_to_all(filter_grad_t, "ctx", 1, 1, tiled=True)

    output = (
        pieces.astype(jnp.float32)
        .reshape(ch_count, block_len, channels)
        .sum(axis=0)
        .astype(jnp.bfloat16)
    )
    return (output, filter_grad)


def solution(mesh):
    return jax.shard_map(
        body,
        mesh=mesh,
        in_specs=(
            P("ctx", "ch"),
            P("ctx", "ch"),
            P("ctx", "ch"),
            P("ch"),
            P("ch", None),
            P("ctx", "ch"),
        ),
        out_specs=(P("ctx", "ch"), P("ctx", "ch")),
        check_vma=False,
    )
```

```python
import functools
import math

import jax
import jax.numpy as jnp
from jax import lax
from jax.experimental import pallas as pl
from jax.experimental.pallas import tpu as pltpu
from jax.sharding import PartitionSpec as P

exact_prec = lax.Precision.HIGHEST


def spectral_tables(block_len):
    time_ids = jnp.arange(2 * block_len, dtype=jnp.int32)
    freq_ids = jnp.arange(block_len, dtype=jnp.int32)
    phase_ids = freq_ids[:, None] * time_ids[None, :] % (2 * block_len)
    angles = phase_ids.astype(jnp.float32) * (math.pi / block_len)
    parity = jnp.where(time_ids % 2 == 0, 1.0, -1.0).astype(jnp.float32)[None, :]
    is_first = (freq_ids == 0)[:, None]
    forward = jnp.concatenate(
        [jnp.cos(angles), jnp.where(is_first, parity, -jnp.sin(angles))], axis=0
    )
    norm_scale = 1.0 / (2 * block_len)
    real_rows = jnp.where(is_first, 1.0, 2.0) * jnp.cos(angles) * norm_scale
    imag_rows = jnp.where(is_first, parity, -2.0 * jnp.sin(angles)) * norm_scale
    inverse = jnp.concatenate([real_rows, imag_rows], axis=0).T
    first_bin = is_first.astype(jnp.float32)
    return (forward, inverse, first_bin)


def spec_product(first_spec, second_spec, first_bin):
    bin_count = first_bin.shape[0]
    first_real, first_imag = (first_spec[..., :bin_count, :], first_spec[..., bin_count:, :])
    second_real, second_imag = (second_spec[..., :bin_count, :], second_spec[..., bin_count:, :])
    others = 1.0 - first_bin
    real_part = first_real * second_real - others * first_imag * second_imag
    imag_part = (
        others * (first_real * second_imag + first_imag * second_real)
        + first_bin * first_imag * second_imag
    )
    return jnp.concatenate([real_part, imag_part], axis=-2)


def conj_product(first_spec, second_spec, first_bin):
    bin_count = first_bin.shape[0]
    first_real, first_imag = (first_spec[..., :bin_count, :], first_spec[..., bin_count:, :])
    second_real, second_imag = (second_spec[..., :bin_count, :], second_spec[..., bin_count:, :])
    others = 1.0 - first_bin
    real_part = first_real * second_real + others * first_imag * second_imag
    imag_part = (
        others * (first_imag * second_real - first_real * second_imag)
        + first_bin * first_imag * second_imag
    )
    return jnp.concatenate([real_part, imag_part], axis=-2)


def transform(dft_table, block_rows):
    return jnp.dot(dft_table, block_rows.astype(jnp.float32), precision=exact_prec)


def shift_blocks(spec, blocks, width):
    if blocks == 0:
        return spec
    rows = spec.shape[0]
    pad = jnp.zeros((rows, blocks * width), spec.dtype)
    return jnp.concatenate([pad, spec[:, : spec.shape[1] - blocks * width]], axis=1)


def conv_products_kernel(width, low_ref, high_ref, taps_ref, conv_ref, seg_ref):
    rows, bins = low_ref.shape
    blocks = rows // width
    half = bins // 2
    for p in range(blocks):
        here = pl.ds(p * width, width)
        if p == 0:
            seg_ref[here, :] = high_ref[here, :]
        else:
            seg_ref[here, :] = high_ref[here, :] + low_ref[pl.ds((p - 1) * width, width), :]
    lane_ids = lax.broadcasted_iota(jnp.int32, (width, half), 1)
    first_bin = lane_ids == 0
    zero = jnp.zeros((width, half), jnp.float32)
    for p in range(blocks):
        acc_re, acc_im = zero, zero
        for k in range(p + 1):
            a_re, a_im = block_parts(taps_ref, k, width)
            b_re, b_im = block_parts(seg_ref, p - k, width)
            both_im = a_im * b_im
            acc_re = acc_re + a_re * b_re - jnp.where(first_bin, 0.0, both_im)
            acc_im = acc_im + jnp.where(first_bin, both_im, a_re * b_im + a_im * b_re)
        conv_ref[pl.ds(p * width, width), :half] = acc_re
        conv_ref[pl.ds(p * width, width), half:] = acc_im


def lag_products_kernel(width, seg_ref, grad_ref, lag_ref):
    rows, bins = seg_ref.shape
    blocks = rows // width
    half = bins // 2
    lane_ids = lax.broadcasted_iota(jnp.int32, (width, half), 1)
    first_bin = lane_ids == 0
    zero = jnp.zeros((width, half), jnp.float32)
    for k in range(blocks):
        acc_re, acc_im = zero, zero
        for p in range(k, blocks):
            a_re, a_im = block_parts(grad_ref, p, width)
            b_re, b_im = block_parts(seg_ref, p - k, width)
            both_im = a_im * b_im
            acc_re = acc_re + a_re * b_re + jnp.where(first_bin, 0.0, both_im)
            acc_im = acc_im + jnp.where(first_bin, both_im, a_im * b_re - a_re * b_im)
        lag_ref[pl.ds(k * width, width), :half] = acc_re
        lag_ref[pl.ds(k * width, width), half:] = acc_im


def block_parts(ref, i, width):
    half = ref.shape[1] // 2
    rows_i = pl.ds(i * width, width)
    return ref[rows_i, :half], ref[rows_i, half:]


def conv_products(low_spec, high_spec, taps_spec, width):
    rows, bins = low_spec.shape
    blocks = rows // width
    vmem = pl.BlockSpec(memory_space=pltpu.VMEM)
    shape = jax.ShapeDtypeStruct(low_spec.shape, jnp.float32)
    return pl.pallas_call(
        functools.partial(conv_products_kernel, width),
        out_shape=(shape, shape),
        in_specs=[vmem, vmem, vmem],
        out_specs=(vmem, vmem),
        cost_estimate=pl.CostEstimate(
            flops=blocks * (blocks + 1) // 2 * width * bins * 4,
            bytes_accessed=5 * rows * bins * 4,
            transcendentals=0,
        ),
    )(low_spec, high_spec, taps_spec)


def lag_products(seg_spec, grad_spec, width):
    rows, bins = seg_spec.shape
    blocks = rows // width
    vmem = pl.BlockSpec(memory_space=pltpu.VMEM)
    return pl.pallas_call(
        functools.partial(lag_products_kernel, width),
        out_shape=jax.ShapeDtypeStruct(seg_spec.shape, jnp.float32),
        in_specs=[vmem, vmem],
        out_specs=vmem,
        cost_estimate=pl.CostEstimate(
            flops=blocks * (blocks + 1) // 2 * width * bins * 4,
            bytes_accessed=3 * rows * bins * 4,
            transcendentals=0,
        ),
    )(seg_spec, grad_spec)


def transform_t(dft_table, block_rows):
    return lax.dot_general(
        block_rows.astype(jnp.float32), dft_table, (((0,), (1,)), ((), ())),
        precision=exact_prec,
    )


def inverse_t(inverse_rows, spec_t):
    return lax.dot_general(
        inverse_rows, spec_t, (((1,), (1,)), ((), ())), precision=exact_prec
    )


def body(inputs, gating, filter_taps, skip_gain, w_out, cotangent):
    block_len, channels = inputs.shape
    ctx_count = lax.axis_size("ctx")
    width = channels // ctx_count
    forward, inverse, first_bin = spectral_tables(block_len)
    first_half = forward[:, :block_len]
    second_half = forward[:, block_len:]

    pair = jnp.stack([inputs, filter_taps])
    pair_t = lax.all_to_all(pair, "ctx", 2, 2, tiled=True)
    signal_t, taps_t = pair_t[0], pair_t[1]

    ch_count = lax.axis_size("ch")
    cot_rows = lax.all_gather(cotangent, "ch", axis=1, tiled=True)
    upstream = lax.dot_general(
        cot_rows,
        w_out,
        (((1,), (1,)), ((), ())),
        preferred_element_type=jnp.float32,
    )
    gate_wide = gating.astype(jnp.float32)
    grad_mixed = upstream * gate_wide
    grad_t = lax.all_to_all(grad_mixed, "ctx", 1, 1, tiled=True)

    conv_spec, seg_spec = conv_products(
        transform_t(first_half, signal_t),
        transform_t(second_half, signal_t),
        transform_t(first_half, taps_t),
        width,
    )

    convolved_t = inverse_t(inverse[block_len:], conv_spec)
    convolved = lax.all_to_all(convolved_t, "ctx", 1, 1, tiled=True)

    mixed_sum = convolved + skip_gain[None, :] * inputs.astype(jnp.float32)
    gated_rows = (gate_wide * mixed_sum).astype(jnp.bfloat16)
    partial_out = jnp.dot(gated_rows, w_out, preferred_element_type=jnp.float32)
    pieces = lax.all_to_all(partial_out.astype(jnp.bfloat16), "ch", 1, 0, tiled=True)

    lag_spec = lag_products(seg_spec, transform_t(second_half, grad_t), width)
    filter_grad_t = inverse_t(inverse[:block_len], lag_spec)
    filter_grad = lax.all_to_all(filter_grad_t, "ctx", 1, 1, tiled=True)

    output = (
        pieces.astype(jnp.float32)
        .reshape(ch_count, block_len, channels)
        .sum(axis=0)
        .astype(jnp.bfloat16)
    )
    return (output, filter_grad)


def solution(mesh):
    return jax.shard_map(
        body,
        mesh=mesh,
        in_specs=(
            P("ctx", "ch"),
            P("ctx", "ch"),
            P("ctx", "ch"),
            P("ch"),
            P("ch", None),
            P("ctx", "ch"),
        ),
        out_specs=(P("ctx", "ch"), P("ctx", "ch")),
        check_vma=False,
    )
```

```python
import functools
import math

import jax
import jax.numpy as jnp
from jax import lax
from jax.experimental import pallas as pl
from jax.experimental.pallas import tpu as pltpu
from jax.sharding import PartitionSpec as P

exact_prec = lax.Precision.HIGHEST


def spectral_tables(block_len):
    time_ids = jnp.arange(2 * block_len, dtype=jnp.int32)
    freq_ids = jnp.arange(block_len, dtype=jnp.int32)
    phase_ids = freq_ids[:, None] * time_ids[None, :] % (2 * block_len)
    angles = phase_ids.astype(jnp.float32) * (math.pi / block_len)
    parity = jnp.where(time_ids % 2 == 0, 1.0, -1.0).astype(jnp.float32)[None, :]
    is_first = (freq_ids == 0)[:, None]
    forward = jnp.concatenate(
        [jnp.cos(angles), jnp.where(is_first, parity, -jnp.sin(angles))], axis=0
    )
    norm_scale = 1.0 / (2 * block_len)
    real_rows = jnp.where(is_first, 1.0, 2.0) * jnp.cos(angles) * norm_scale
    imag_rows = jnp.where(is_first, parity, -2.0 * jnp.sin(angles)) * norm_scale
    inverse = jnp.concatenate([real_rows, imag_rows], axis=0).T
    first_bin = is_first.astype(jnp.float32)
    return (forward, inverse, first_bin)


def spec_product(first_spec, second_spec, first_bin):
    bin_count = first_bin.shape[0]
    first_real, first_imag = (first_spec[..., :bin_count, :], first_spec[..., bin_count:, :])
    second_real, second_imag = (second_spec[..., :bin_count, :], second_spec[..., bin_count:, :])
    others = 1.0 - first_bin
    real_part = first_real * second_real - others * first_imag * second_imag
    imag_part = (
        others * (first_real * second_imag + first_imag * second_real)
        + first_bin * first_imag * second_imag
    )
    return jnp.concatenate([real_part, imag_part], axis=-2)


def conj_product(first_spec, second_spec, first_bin):
    bin_count = first_bin.shape[0]
    first_real, first_imag = (first_spec[..., :bin_count, :], first_spec[..., bin_count:, :])
    second_real, second_imag = (second_spec[..., :bin_count, :], second_spec[..., bin_count:, :])
    others = 1.0 - first_bin
    real_part = first_real * second_real + others * first_imag * second_imag
    imag_part = (
        others * (first_imag * second_real - first_real * second_imag)
        + first_bin * first_imag * second_imag
    )
    return jnp.concatenate([real_part, imag_part], axis=-2)


def transform(dft_table, block_rows):
    return jnp.dot(dft_table, block_rows.astype(jnp.float32), precision=exact_prec)


def shift_blocks(spec, blocks, width):
    if blocks == 0:
        return spec
    rows = spec.shape[0]
    pad = jnp.zeros((rows, blocks * width), spec.dtype)
    return jnp.concatenate([pad, spec[:, : spec.shape[1] - blocks * width]], axis=1)


def conv_products_kernel(width, low_ref, high_ref, taps_ref, conv_ref, seg_ref):
    rows, bins = low_ref.shape
    blocks = rows // width
    half = bins // 2
    for p in range(blocks):
        here = pl.ds(p * width, width)
        if p == 0:
            seg_ref[here, :] = high_ref[here, :]
        else:
            seg_ref[here, :] = high_ref[here, :] + low_ref[pl.ds((p - 1) * width, width), :]
    lane_ids = lax.broadcasted_iota(jnp.int32, (width, half), 1)
    first_bin = lane_ids == 0
    zero = jnp.zeros((width, half), jnp.float32)
    for p in range(blocks):
        acc_re, acc_im = zero, zero
        for k in range(p + 1):
            a_re, a_im = block_parts(taps_ref, k, width)
            b_re, b_im = block_parts(seg_ref, p - k, width)
            both_im = a_im * b_im
            acc_re = acc_re + a_re * b_re - jnp.where(first_bin, 0.0, both_im)
            acc_im = acc_im + jnp.where(first_bin, both_im, a_re * b_im + a_im * b_re)
        conv_ref[pl.ds(p * width, width), :half] = acc_re
        conv_ref[pl.ds(p * width, width), half:] = acc_im


def lag_products_kernel(width, seg_ref, grad_ref, lag_ref):
    rows, bins = seg_ref.shape
    blocks = rows // width
    half = bins // 2
    lane_ids = lax.broadcasted_iota(jnp.int32, (width, half), 1)
    first_bin = lane_ids == 0
    zero = jnp.zeros((width, half), jnp.float32)
    for k in range(blocks):
        acc_re, acc_im = zero, zero
        for p in range(k, blocks):
            a_re, a_im = block_parts(grad_ref, p, width)
            b_re, b_im = block_parts(seg_ref, p - k, width)
            both_im = a_im * b_im
            acc_re = acc_re + a_re * b_re + jnp.where(first_bin, 0.0, both_im)
            acc_im = acc_im + jnp.where(first_bin, both_im, a_im * b_re - a_re * b_im)
        lag_ref[pl.ds(k * width, width), :half] = acc_re
        lag_ref[pl.ds(k * width, width), half:] = acc_im


def block_parts(ref, i, width):
    half = ref.shape[1] // 2
    rows_i = pl.ds(i * width, width)
    return ref[rows_i, :half], ref[rows_i, half:]


def conv_products(low_spec, high_spec, taps_spec, width):
    rows, bins = low_spec.shape
    blocks = rows // width
    vmem = pl.BlockSpec(memory_space=pltpu.VMEM)
    shape = jax.ShapeDtypeStruct(low_spec.shape, jnp.float32)
    return pl.pallas_call(
        functools.partial(conv_products_kernel, width),
        out_shape=(shape, shape),
        in_specs=[vmem, vmem, vmem],
        out_specs=(vmem, vmem),
        cost_estimate=pl.CostEstimate(
            flops=blocks * (blocks + 1) // 2 * width * bins * 4,
            bytes_accessed=5 * rows * bins * 4,
            transcendentals=0,
        ),
    )(low_spec, high_spec, taps_spec)


def lag_products(seg_spec, grad_spec, width):
    rows, bins = seg_spec.shape
    blocks = rows // width
    vmem = pl.BlockSpec(memory_space=pltpu.VMEM)
    return pl.pallas_call(
        functools.partial(lag_products_kernel, width),
        out_shape=jax.ShapeDtypeStruct(seg_spec.shape, jnp.float32),
        in_specs=[vmem, vmem],
        out_specs=vmem,
        cost_estimate=pl.CostEstimate(
            flops=blocks * (blocks + 1) // 2 * width * bins * 4,
            bytes_accessed=3 * rows * bins * 4,
            transcendentals=0,
        ),
    )(seg_spec, grad_spec)


def transform_t(dft_table, block_rows):
    return lax.dot_general(
        block_rows.astype(jnp.float32), dft_table, (((0,), (1,)), ((), ())),
        precision=exact_prec,
    )


def inverse_t(inverse_rows, spec_t):
    return lax.dot_general(
        inverse_rows, spec_t, (((1,), (1,)), ((), ())), precision=exact_prec
    )


def body(inputs, gating, filter_taps, skip_gain, w_out, cotangent):
    block_len, channels = inputs.shape
    ctx_count = lax.axis_size("ctx")
    width = channels // ctx_count
    forward, inverse, first_bin = spectral_tables(block_len)
    first_half = forward[:, :block_len]
    second_half = forward[:, block_len:]

    pair = jnp.stack([inputs, filter_taps])
    pair_t = lax.all_to_all(pair, "ctx", 2, 2, tiled=True)
    signal_t, taps_t = pair_t[0], pair_t[1]

    ch_count = lax.axis_size("ch")
    cot_rows = lax.all_gather(cotangent, "ch", axis=1, tiled=True)
    upstream = lax.dot_general(
        cot_rows,
        w_out,
        (((1,), (1,)), ((), ())),
        preferred_element_type=jnp.float32,
    )
    gate_wide = gating.astype(jnp.float32)
    grad_mixed = upstream * gate_wide

    conv_spec, seg_spec = conv_products(
        transform_t(first_half, signal_t),
        transform_t(second_half, signal_t),
        transform_t(first_half, taps_t),
        width,
    )

    convolved_t = inverse_t(inverse[block_len:], conv_spec)
    convolved = lax.all_to_all(convolved_t, "ctx", 1, 1, tiled=True)

    mixed_sum = convolved + skip_gain[None, :] * inputs.astype(jnp.float32)
    gated_rows = (gate_wide * mixed_sum).astype(jnp.bfloat16)
    partial_out = jnp.dot(gated_rows, w_out, preferred_element_type=jnp.float32)
    pieces = lax.all_to_all(partial_out.astype(jnp.bfloat16), "ch", 1, 0, tiled=True)
    pieces, grad_mixed = lax.optimization_barrier((pieces, grad_mixed))
    grad_t = lax.all_to_all(grad_mixed, "ctx", 1, 1, tiled=True)

    lag_spec = lag_products(seg_spec, transform_t(second_half, grad_t), width)
    filter_grad_t = inverse_t(inverse[:block_len], lag_spec)
    filter_grad = lax.all_to_all(filter_grad_t, "ctx", 1, 1, tiled=True)

    output = (
        pieces.astype(jnp.float32)
        .reshape(ch_count, block_len, channels)
        .sum(axis=0)
        .astype(jnp.bfloat16)
    )
    return (output, filter_grad)


def solution(mesh):
    return jax.shard_map(
        body,
        mesh=mesh,
        in_specs=(
            P("ctx", "ch"),
            P("ctx", "ch"),
            P("ctx", "ch"),
            P("ch"),
            P("ch", None),
            P("ctx", "ch"),
        ),
        out_specs=(P("ctx", "ch"), P("ctx", "ch")),
        check_vma=False,
    )
```

```python
import functools
import math

import jax
import jax.numpy as jnp
from jax import lax
from jax.experimental import pallas as pl
from jax.experimental.pallas import tpu as pltpu
from jax.sharding import PartitionSpec as P

exact_prec = lax.Precision.HIGHEST


def spectral_tables(block_len):
    time_ids = jnp.arange(2 * block_len, dtype=jnp.int32)
    freq_ids = jnp.arange(block_len, dtype=jnp.int32)
    phase_ids = freq_ids[:, None] * time_ids[None, :] % (2 * block_len)
    angles = phase_ids.astype(jnp.float32) * (math.pi / block_len)
    parity = jnp.where(time_ids % 2 == 0, 1.0, -1.0).astype(jnp.float32)[None, :]
    is_first = (freq_ids == 0)[:, None]
    forward = jnp.concatenate(
        [jnp.cos(angles), jnp.where(is_first, parity, -jnp.sin(angles))], axis=0
    )
    norm_scale = 1.0 / (2 * block_len)
    real_rows = jnp.where(is_first, 1.0, 2.0) * jnp.cos(angles) * norm_scale
    imag_rows = jnp.where(is_first, parity, -2.0 * jnp.sin(angles)) * norm_scale
    inverse = jnp.concatenate([real_rows, imag_rows], axis=0).T
    first_bin = is_first.astype(jnp.float32)
    return (forward, inverse, first_bin)


def spec_product(first_spec, second_spec, first_bin):
    bin_count = first_bin.shape[0]
    first_real, first_imag = (first_spec[..., :bin_count, :], first_spec[..., bin_count:, :])
    second_real, second_imag = (second_spec[..., :bin_count, :], second_spec[..., bin_count:, :])
    others = 1.0 - first_bin
    real_part = first_real * second_real - others * first_imag * second_imag
    imag_part = (
        others * (first_real * second_imag + first_imag * second_real)
        + first_bin * first_imag * second_imag
    )
    return jnp.concatenate([real_part, imag_part], axis=-2)


def conj_product(first_spec, second_spec, first_bin):
    bin_count = first_bin.shape[0]
    first_real, first_imag = (first_spec[..., :bin_count, :], first_spec[..., bin_count:, :])
    second_real, second_imag = (second_spec[..., :bin_count, :], second_spec[..., bin_count:, :])
    others = 1.0 - first_bin
    real_part = first_real * second_real + others * first_imag * second_imag
    imag_part = (
        others * (first_imag * second_real - first_real * second_imag)
        + first_bin * first_imag * second_imag
    )
    return jnp.concatenate([real_part, imag_part], axis=-2)


def transform(dft_table, block_rows):
    return jnp.dot(dft_table, block_rows.astype(jnp.float32), precision=exact_prec)


def shift_blocks(spec, blocks, width):
    if blocks == 0:
        return spec
    rows = spec.shape[0]
    pad = jnp.zeros((rows, blocks * width), spec.dtype)
    return jnp.concatenate([pad, spec[:, : spec.shape[1] - blocks * width]], axis=1)


def conv_products_kernel(width, low_ref, high_ref, taps_ref, conv_ref, seg_ref):
    rows, bins = low_ref.shape
    blocks = rows // width
    half = bins // 2
    for p in range(blocks):
        here = pl.ds(p * width, width)
        if p == 0:
            seg_ref[here, :] = high_ref[here, :]
        else:
            seg_ref[here, :] = high_ref[here, :] + low_ref[pl.ds((p - 1) * width, width), :]
    lane_ids = lax.broadcasted_iota(jnp.int32, (width, half), 1)
    first_bin = lane_ids == 0
    zero = jnp.zeros((width, half), jnp.float32)
    for p in range(blocks):
        acc_re, acc_im = zero, zero
        for k in range(p + 1):
            a_re, a_im = block_parts(taps_ref, k, width)
            b_re, b_im = block_parts(seg_ref, p - k, width)
            both_im = a_im * b_im
            acc_re = acc_re + a_re * b_re - jnp.where(first_bin, 0.0, both_im)
            acc_im = acc_im + jnp.where(first_bin, both_im, a_re * b_im + a_im * b_re)
        conv_ref[pl.ds(p * width, width), :half] = acc_re
        conv_ref[pl.ds(p * width, width), half:] = acc_im


def lag_products_kernel(width, seg_ref, grad_ref, lag_ref):
    rows, bins = seg_ref.shape
    blocks = rows // width
    half = bins // 2
    lane_ids = lax.broadcasted_iota(jnp.int32, (width, half), 1)
    first_bin = lane_ids == 0
    zero = jnp.zeros((width, half), jnp.float32)
    for k in range(blocks):
        acc_re, acc_im = zero, zero
        for p in range(k, blocks):
            a_re, a_im = block_parts(grad_ref, p, width)
            b_re, b_im = block_parts(seg_ref, p - k, width)
            both_im = a_im * b_im
            acc_re = acc_re + a_re * b_re + jnp.where(first_bin, 0.0, both_im)
            acc_im = acc_im + jnp.where(first_bin, both_im, a_im * b_re - a_re * b_im)
        lag_ref[pl.ds(k * width, width), :half] = acc_re
        lag_ref[pl.ds(k * width, width), half:] = acc_im


def block_parts(ref, i, width):
    half = ref.shape[1] // 2
    rows_i = pl.ds(i * width, width)
    return ref[rows_i, :half], ref[rows_i, half:]


def conv_products(low_spec, high_spec, taps_spec, width):
    rows, bins = low_spec.shape
    blocks = rows // width
    vmem = pl.BlockSpec(memory_space=pltpu.VMEM)
    shape = jax.ShapeDtypeStruct(low_spec.shape, jnp.float32)
    return pl.pallas_call(
        functools.partial(conv_products_kernel, width),
        out_shape=(shape, shape),
        in_specs=[vmem, vmem, vmem],
        out_specs=(vmem, vmem),
        cost_estimate=pl.CostEstimate(
            flops=blocks * (blocks + 1) // 2 * width * bins * 4,
            bytes_accessed=5 * rows * bins * 4,
            transcendentals=0,
        ),
    )(low_spec, high_spec, taps_spec)


def lag_products(seg_spec, grad_spec, width):
    rows, bins = seg_spec.shape
    blocks = rows // width
    vmem = pl.BlockSpec(memory_space=pltpu.VMEM)
    return pl.pallas_call(
        functools.partial(lag_products_kernel, width),
        out_shape=jax.ShapeDtypeStruct(seg_spec.shape, jnp.float32),
        in_specs=[vmem, vmem],
        out_specs=vmem,
        cost_estimate=pl.CostEstimate(
            flops=blocks * (blocks + 1) // 2 * width * bins * 4,
            bytes_accessed=3 * rows * bins * 4,
            transcendentals=0,
        ),
    )(seg_spec, grad_spec)


def transform_t(dft_table, block_rows):
    return lax.dot_general(
        block_rows.astype(jnp.float32), dft_table, (((0,), (1,)), ((), ())),
        precision=exact_prec,
    )


def inverse_t(inverse_rows, spec_t):
    return lax.dot_general(
        inverse_rows, spec_t, (((1,), (1,)), ((), ())), precision=exact_prec
    )


def body(inputs, gating, filter_taps, skip_gain, w_out, cotangent):
    block_len, channels = inputs.shape
    ctx_count = lax.axis_size("ctx")
    width = channels // ctx_count
    forward, inverse, first_bin = spectral_tables(block_len)
    first_half = forward[:, :block_len]
    second_half = forward[:, block_len:]

    pair = jnp.stack([inputs, filter_taps])
    pair_t = lax.all_to_all(pair, "ctx", 2, 2, tiled=True)
    signal_t, taps_t = pair_t[0], pair_t[1]

    ch_count = lax.axis_size("ch")
    cot_copies = jnp.tile(cotangent, (1, ch_count))
    pair_t, cot_copies = lax.optimization_barrier((pair_t, cot_copies))
    signal_t, taps_t = pair_t[0], pair_t[1]
    cot_rows = lax.all_to_all(cot_copies, "ch", 1, 1, tiled=True)
    gate_wide = gating.astype(jnp.float32)

    conv_spec, seg_spec = conv_products(
        transform_t(first_half, signal_t),
        transform_t(second_half, signal_t),
        transform_t(first_half, taps_t),
        width,
    )

    conv_spec, cot_rows = lax.optimization_barrier((conv_spec, cot_rows))
    convolved_t = inverse_t(inverse[block_len:], conv_spec)
    upstream = lax.dot_general(
        cot_rows,
        w_out,
        (((1,), (1,)), ((), ())),
        preferred_element_type=jnp.float32,
    )
    grad_mixed = upstream * gate_wide
    convolved = lax.all_to_all(convolved_t, "ctx", 1, 1, tiled=True)

    mixed_sum = convolved + skip_gain[None, :] * inputs.astype(jnp.float32)
    gated_rows = (gate_wide * mixed_sum).astype(jnp.bfloat16)
    partial_out = jnp.dot(gated_rows, w_out, preferred_element_type=jnp.float32)
    pieces = lax.all_to_all(partial_out.astype(jnp.bfloat16), "ch", 1, 0, tiled=True)
    pieces, grad_mixed = lax.optimization_barrier((pieces, grad_mixed))
    grad_t = lax.all_to_all(grad_mixed, "ctx", 1, 1, tiled=True)

    lag_spec = lag_products(seg_spec, transform_t(second_half, grad_t), width)
    filter_grad_t = inverse_t(inverse[:block_len], lag_spec)
    filter_grad = lax.all_to_all(filter_grad_t, "ctx", 1, 1, tiled=True)

    output = (
        pieces.astype(jnp.float32)
        .reshape(ch_count, block_len, channels)
        .sum(axis=0)
        .astype(jnp.bfloat16)
    )
    return (output, filter_grad)


def solution(mesh):
    return jax.shard_map(
        body,
        mesh=mesh,
        in_specs=(
            P("ctx", "ch"),
            P("ctx", "ch"),
            P("ctx", "ch"),
            P("ch"),
            P("ch", None),
            P("ctx", "ch"),
        ),
        out_specs=(P("ctx", "ch"), P("ctx", "ch")),
        check_vma=False,
    )
```

```python
import functools
import math

import jax
import jax.numpy as jnp
from jax import lax
from jax.experimental import pallas as pl
from jax.experimental.pallas import tpu as pltpu
from jax.sharding import PartitionSpec as P

exact_prec = lax.Precision.HIGHEST


def spectral_tables(block_len):
    time_ids = jnp.arange(2 * block_len, dtype=jnp.int32)
    freq_ids = jnp.arange(block_len, dtype=jnp.int32)
    phase_ids = freq_ids[:, None] * time_ids[None, :] % (2 * block_len)
    angles = phase_ids.astype(jnp.float32) * (math.pi / block_len)
    parity = jnp.where(time_ids % 2 == 0, 1.0, -1.0).astype(jnp.float32)[None, :]
    is_first = (freq_ids == 0)[:, None]
    forward = jnp.concatenate(
        [jnp.cos(angles), jnp.where(is_first, parity, -jnp.sin(angles))], axis=0
    )
    norm_scale = 1.0 / (2 * block_len)
    real_rows = jnp.where(is_first, 1.0, 2.0) * jnp.cos(angles) * norm_scale
    imag_rows = jnp.where(is_first, parity, -2.0 * jnp.sin(angles)) * norm_scale
    inverse = jnp.concatenate([real_rows, imag_rows], axis=0).T
    first_bin = is_first.astype(jnp.float32)
    return (forward, inverse, first_bin)


def spec_product(first_spec, second_spec, first_bin):
    bin_count = first_bin.shape[0]
    first_real, first_imag = (first_spec[..., :bin_count, :], first_spec[..., bin_count:, :])
    second_real, second_imag = (second_spec[..., :bin_count, :], second_spec[..., bin_count:, :])
    others = 1.0 - first_bin
    real_part = first_real * second_real - others * first_imag * second_imag
    imag_part = (
        others * (first_real * second_imag + first_imag * second_real)
        + first_bin * first_imag * second_imag
    )
    return jnp.concatenate([real_part, imag_part], axis=-2)


def conj_product(first_spec, second_spec, first_bin):
    bin_count = first_bin.shape[0]
    first_real, first_imag = (first_spec[..., :bin_count, :], first_spec[..., bin_count:, :])
    second_real, second_imag = (second_spec[..., :bin_count, :], second_spec[..., bin_count:, :])
    others = 1.0 - first_bin
    real_part = first_real * second_real + others * first_imag * second_imag
    imag_part = (
        others * (first_imag * second_real - first_real * second_imag)
        + first_bin * first_imag * second_imag
    )
    return jnp.concatenate([real_part, imag_part], axis=-2)


def transform(dft_table, block_rows):
    return jnp.dot(dft_table, block_rows.astype(jnp.float32), precision=exact_prec)


def shift_blocks(spec, blocks, width):
    if blocks == 0:
        return spec
    rows = spec.shape[0]
    pad = jnp.zeros((rows, blocks * width), spec.dtype)
    return jnp.concatenate([pad, spec[:, : spec.shape[1] - blocks * width]], axis=1)


def conv_products_kernel(width, low_ref, high_ref, taps_ref, conv_ref, seg_ref):
    rows, bins = low_ref.shape
    blocks = rows // width
    half = bins // 2
    for p in range(blocks):
        here = pl.ds(p * width, width)
        if p == 0:
            seg_ref[here, :] = high_ref[here, :]
        else:
            seg_ref[here, :] = high_ref[here, :] + low_ref[pl.ds((p - 1) * width, width), :]
    lane_ids = lax.broadcasted_iota(jnp.int32, (width, half), 1)
    first_bin = lane_ids == 0
    zero = jnp.zeros((width, half), jnp.float32)
    for p in range(blocks):
        acc_re, acc_im = zero, zero
        for k in range(p + 1):
            a_re, a_im = block_parts(taps_ref, k, width)
            b_re, b_im = block_parts(seg_ref, p - k, width)
            both_im = a_im * b_im
            acc_re = acc_re + a_re * b_re - jnp.where(first_bin, 0.0, both_im)
            acc_im = acc_im + jnp.where(first_bin, both_im, a_re * b_im + a_im * b_re)
        conv_ref[pl.ds(p * width, width), :half] = acc_re
        conv_ref[pl.ds(p * width, width), half:] = acc_im


def lag_products_kernel(width, seg_ref, grad_ref, lag_ref):
    rows, bins = seg_ref.shape
    blocks = rows // width
    half = bins // 2
    lane_ids = lax.broadcasted_iota(jnp.int32, (width, half), 1)
    first_bin = lane_ids == 0
    zero = jnp.zeros((width, half), jnp.float32)
    for k in range(blocks):
        acc_re, acc_im = zero, zero
        for p in range(k, blocks):
            a_re, a_im = block_parts(grad_ref, p, width)
            b_re, b_im = block_parts(seg_ref, p - k, width)
            both_im = a_im * b_im
            acc_re = acc_re + a_re * b_re + jnp.where(first_bin, 0.0, both_im)
            acc_im = acc_im + jnp.where(first_bin, both_im, a_im * b_re - a_re * b_im)
        lag_ref[pl.ds(k * width, width), :half] = acc_re
        lag_ref[pl.ds(k * width, width), half:] = acc_im


def block_parts(ref, i, width):
    half = ref.shape[1] // 2
    rows_i = pl.ds(i * width, width)
    return ref[rows_i, :half], ref[rows_i, half:]


def conv_products(low_spec, high_spec, taps_spec, width):
    rows, bins = low_spec.shape
    blocks = rows // width
    vmem = pl.BlockSpec(memory_space=pltpu.VMEM)
    shape = jax.ShapeDtypeStruct(low_spec.shape, jnp.float32)
    return pl.pallas_call(
        functools.partial(conv_products_kernel, width),
        out_shape=(shape, shape),
        in_specs=[vmem, vmem, vmem],
        out_specs=(vmem, vmem),
        cost_estimate=pl.CostEstimate(
            flops=blocks * (blocks + 1) // 2 * width * bins * 4,
            bytes_accessed=5 * rows * bins * 4,
            transcendentals=0,
        ),
    )(low_spec, high_spec, taps_spec)


def lag_products(seg_spec, grad_spec, width):
    rows, bins = seg_spec.shape
    blocks = rows // width
    vmem = pl.BlockSpec(memory_space=pltpu.VMEM)
    return pl.pallas_call(
        functools.partial(lag_products_kernel, width),
        out_shape=jax.ShapeDtypeStruct(seg_spec.shape, jnp.float32),
        in_specs=[vmem, vmem],
        out_specs=vmem,
        cost_estimate=pl.CostEstimate(
            flops=blocks * (blocks + 1) // 2 * width * bins * 4,
            bytes_accessed=3 * rows * bins * 4,
            transcendentals=0,
        ),
    )(seg_spec, grad_spec)


def transform_t(dft_table, block_rows):
    return lax.dot_general(
        block_rows.astype(jnp.float32), dft_table, (((1,), (1,)), ((), ())),
        precision=exact_prec,
    )


def inverse_t(inverse_rows, spec_t):
    return lax.dot_general(
        spec_t, inverse_rows, (((1,), (1,)), ((), ())), precision=exact_prec
    )


def body(inputs, gating, filter_taps, skip_gain, w_out, cotangent):
    block_len, channels = inputs.shape
    ctx_count = lax.axis_size("ctx")
    width = channels // ctx_count
    forward, inverse, first_bin = spectral_tables(block_len)
    first_half = forward[:, :block_len]
    second_half = forward[:, block_len:]

    pair = jnp.stack([inputs.T, filter_taps.T])
    pair_t = lax.all_to_all(pair, "ctx", 1, 1, tiled=True)
    signal_t, taps_t = pair_t[0], pair_t[1]

    ch_count = lax.axis_size("ch")
    cot_rows = lax.all_gather(cotangent, "ch", axis=1, tiled=True)
    upstream = lax.dot_general(
        cot_rows,
        w_out,
        (((1,), (1,)), ((), ())),
        preferred_element_type=jnp.float32,
    )
    gate_wide = gating.astype(jnp.float32)
    grad_mixed = upstream * gate_wide

    conv_spec, seg_spec = conv_products(
        transform_t(first_half, signal_t),
        transform_t(second_half, signal_t),
        transform_t(first_half, taps_t),
        width,
    )

    convolved_t = inverse_t(inverse[block_len:], conv_spec)
    convolved = lax.all_to_all(convolved_t, "ctx", 0, 0, tiled=True).T

    mixed_sum = convolved + skip_gain[None, :] * inputs.astype(jnp.float32)
    gated_rows = (gate_wide * mixed_sum).astype(jnp.bfloat16)
    partial_out = jnp.dot(gated_rows, w_out, preferred_element_type=jnp.float32)
    pieces = lax.all_to_all(partial_out.astype(jnp.bfloat16), "ch", 1, 0, tiled=True)
    pieces, grad_mixed = lax.optimization_barrier((pieces, grad_mixed))
    grad_t = lax.all_to_all(grad_mixed.T, "ctx", 0, 0, tiled=True)

    lag_spec = lag_products(seg_spec, transform_t(second_half, grad_t), width)
    filter_grad_t = inverse_t(inverse[:block_len], lag_spec)
    filter_grad = lax.all_to_all(filter_grad_t, "ctx", 0, 0, tiled=True).T

    output = (
        pieces.astype(jnp.float32)
        .reshape(ch_count, block_len, channels)
        .sum(axis=0)
        .astype(jnp.bfloat16)
    )
    return (output, filter_grad)


def solution(mesh):
    return jax.shard_map(
        body,
        mesh=mesh,
        in_specs=(
            P("ctx", "ch"),
            P("ctx", "ch"),
            P("ctx", "ch"),
            P("ch"),
            P("ch", None),
            P("ctx", "ch"),
        ),
        out_specs=(P("ctx", "ch"), P("ctx", "ch")),
        check_vma=False,
    )
```

```python
import functools
import math

import jax
import jax.numpy as jnp
from jax import lax
from jax.experimental import pallas as pl
from jax.experimental.pallas import tpu as pltpu
from jax.sharding import PartitionSpec as P

exact_prec = lax.Precision.HIGHEST


def spectral_tables(block_len):
    time_ids = jnp.arange(2 * block_len, dtype=jnp.int32)
    freq_ids = jnp.arange(block_len, dtype=jnp.int32)
    phase_ids = freq_ids[:, None] * time_ids[None, :] % (2 * block_len)
    angles = phase_ids.astype(jnp.float32) * (math.pi / block_len)
    parity = jnp.where(time_ids % 2 == 0, 1.0, -1.0).astype(jnp.float32)[None, :]
    is_first = (freq_ids == 0)[:, None]
    forward = jnp.concatenate(
        [jnp.cos(angles), jnp.where(is_first, parity, -jnp.sin(angles))], axis=0
    )
    norm_scale = 1.0 / (2 * block_len)
    real_rows = jnp.where(is_first, 1.0, 2.0) * jnp.cos(angles) * norm_scale
    imag_rows = jnp.where(is_first, parity, -2.0 * jnp.sin(angles)) * norm_scale
    inverse = jnp.concatenate([real_rows, imag_rows], axis=0).T
    first_bin = is_first.astype(jnp.float32)
    return (forward, inverse, first_bin)


def spec_product(first_spec, second_spec, first_bin):
    bin_count = first_bin.shape[0]
    first_real, first_imag = (first_spec[..., :bin_count, :], first_spec[..., bin_count:, :])
    second_real, second_imag = (second_spec[..., :bin_count, :], second_spec[..., bin_count:, :])
    others = 1.0 - first_bin
    real_part = first_real * second_real - others * first_imag * second_imag
    imag_part = (
        others * (first_real * second_imag + first_imag * second_real)
        + first_bin * first_imag * second_imag
    )
    return jnp.concatenate([real_part, imag_part], axis=-2)


def conj_product(first_spec, second_spec, first_bin):
    bin_count = first_bin.shape[0]
    first_real, first_imag = (first_spec[..., :bin_count, :], first_spec[..., bin_count:, :])
    second_real, second_imag = (second_spec[..., :bin_count, :], second_spec[..., bin_count:, :])
    others = 1.0 - first_bin
    real_part = first_real * second_real + others * first_imag * second_imag
    imag_part = (
        others * (first_imag * second_real - first_real * second_imag)
        + first_bin * first_imag * second_imag
    )
    return jnp.concatenate([real_part, imag_part], axis=-2)


def transform(dft_table, block_rows):
    return jnp.dot(dft_table, block_rows.astype(jnp.float32), precision=exact_prec)


def shift_blocks(spec, blocks, width):
    if blocks == 0:
        return spec
    rows = spec.shape[0]
    pad = jnp.zeros((rows, blocks * width), spec.dtype)
    return jnp.concatenate([pad, spec[:, : spec.shape[1] - blocks * width]], axis=1)


def conv_products_kernel(width, low_ref, high_ref, taps_ref, conv_ref, seg_ref):
    rows, bins = low_ref.shape
    blocks = rows // width
    half = bins // 2
    for p in range(blocks):
        here = pl.ds(p * width, width)
        if p == 0:
            seg_ref[here, :] = high_ref[here, :]
        else:
            seg_ref[here, :] = high_ref[here, :] + low_ref[pl.ds((p - 1) * width, width), :]
    lane_ids = lax.broadcasted_iota(jnp.int32, (width, half), 1)
    first_bin = lane_ids == 0
    zero = jnp.zeros((width, half), jnp.float32)
    for p in range(blocks):
        acc_re, acc_im = zero, zero
        for k in range(p + 1):
            a_re, a_im = block_parts(taps_ref, k, width)
            b_re, b_im = block_parts(seg_ref, p - k, width)
            both_im = a_im * b_im
            acc_re = acc_re + a_re * b_re - jnp.where(first_bin, 0.0, both_im)
            acc_im = acc_im + jnp.where(first_bin, both_im, a_re * b_im + a_im * b_re)
        conv_ref[pl.ds(p * width, width), :half] = acc_re
        conv_ref[pl.ds(p * width, width), half:] = acc_im


def lag_products_kernel(width, seg_ref, grad_ref, lag_ref):
    rows, bins = seg_ref.shape
    blocks = rows // width
    half = bins // 2
    lane_ids = lax.broadcasted_iota(jnp.int32, (width, half), 1)
    first_bin = lane_ids == 0
    zero = jnp.zeros((width, half), jnp.float32)
    for k in range(blocks):
        acc_re, acc_im = zero, zero
        for p in range(k, blocks):
            a_re, a_im = block_parts(grad_ref, p, width)
            b_re, b_im = block_parts(seg_ref, p - k, width)
            both_im = a_im * b_im
            acc_re = acc_re + a_re * b_re + jnp.where(first_bin, 0.0, both_im)
            acc_im = acc_im + jnp.where(first_bin, both_im, a_im * b_re - a_re * b_im)
        lag_ref[pl.ds(k * width, width), :half] = acc_re
        lag_ref[pl.ds(k * width, width), half:] = acc_im


def block_parts(ref, i, width):
    half = ref.shape[1] // 2
    rows_i = pl.ds(i * width, width)
    return ref[rows_i, :half], ref[rows_i, half:]


def conv_products(low_spec, high_spec, taps_spec, width):
    rows, bins = low_spec.shape
    blocks = rows // width
    vmem = pl.BlockSpec(memory_space=pltpu.VMEM)
    shape = jax.ShapeDtypeStruct(low_spec.shape, jnp.float32)
    return pl.pallas_call(
        functools.partial(conv_products_kernel, width),
        out_shape=(shape, shape),
        in_specs=[vmem, vmem, vmem],
        out_specs=(vmem, vmem),
        cost_estimate=pl.CostEstimate(
            flops=blocks * (blocks + 1) // 2 * width * bins * 4,
            bytes_accessed=5 * rows * bins * 4,
            transcendentals=0,
        ),
    )(low_spec, high_spec, taps_spec)


def lag_products(seg_spec, grad_spec, width):
    rows, bins = seg_spec.shape
    blocks = rows // width
    vmem = pl.BlockSpec(memory_space=pltpu.VMEM)
    return pl.pallas_call(
        functools.partial(lag_products_kernel, width),
        out_shape=jax.ShapeDtypeStruct(seg_spec.shape, jnp.float32),
        in_specs=[vmem, vmem],
        out_specs=vmem,
        cost_estimate=pl.CostEstimate(
            flops=blocks * (blocks + 1) // 2 * width * bins * 4,
            bytes_accessed=3 * rows * bins * 4,
            transcendentals=0,
        ),
    )(seg_spec, grad_spec)


def transform_t(dft_table, block_rows):
    return lax.dot_general(
        block_rows.astype(jnp.float32), dft_table, (((1,), (1,)), ((), ())),
        precision=exact_prec,
    )


def inverse_t(inverse_rows, spec_t):
    return lax.dot_general(
        spec_t, inverse_rows, (((1,), (1,)), ((), ())), precision=exact_prec
    )


def body(inputs, gating, filter_taps, skip_gain, w_out, cotangent):
    block_len, channels = inputs.shape
    ctx_count = lax.axis_size("ctx")
    width = channels // ctx_count
    forward, inverse, first_bin = spectral_tables(block_len)
    first_half = forward[:, :block_len]
    second_half = forward[:, block_len:]

    pair = jnp.stack([inputs.T, filter_taps.T])
    pair_t = lax.all_to_all(pair, "ctx", 1, 1, tiled=True)
    signal_t, taps_t = pair_t[0], pair_t[1]

    ch_count = lax.axis_size("ch")
    cot_rows = lax.all_gather(cotangent, "ch", axis=1, tiled=True)
    upstream = lax.dot_general(
        cot_rows,
        w_out,
        (((1,), (1,)), ((), ())),
        preferred_element_type=jnp.float32,
    )
    gate_wide = gating.astype(jnp.float32)
    grad_mixed = upstream * gate_wide

    conv_spec, seg_spec = conv_products(
        transform_t(first_half, signal_t),
        transform_t(second_half, signal_t),
        transform_t(first_half, taps_t),
        width,
    )

    convolved_t = inverse_t(inverse[block_len:], conv_spec)
    convolved = lax.all_to_all(
        convolved_t.astype(jnp.bfloat16), "ctx", 0, 0, tiled=True
    ).T.astype(jnp.float32)

    mixed_sum = convolved + skip_gain[None, :] * inputs.astype(jnp.float32)
    gated_rows = (gate_wide * mixed_sum).astype(jnp.bfloat16)
    partial_out = jnp.dot(gated_rows, w_out, preferred_element_type=jnp.float32)
    pieces = lax.all_to_all(partial_out.astype(jnp.bfloat16), "ch", 1, 0, tiled=True)
    pieces, grad_mixed = lax.optimization_barrier((pieces, grad_mixed))
    grad_t = lax.all_to_all(grad_mixed.T.astype(jnp.bfloat16), "ctx", 0, 0, tiled=True)

    lag_spec = lag_products(seg_spec, transform_t(second_half, grad_t), width)
    filter_grad_t = inverse_t(inverse[:block_len], lag_spec)
    filter_grad = lax.all_to_all(
        filter_grad_t.astype(jnp.bfloat16), "ctx", 0, 0, tiled=True
    ).T.astype(jnp.float32)

    output = (
        pieces.astype(jnp.float32)
        .reshape(ch_count, block_len, channels)
        .sum(axis=0)
        .astype(jnp.bfloat16)
    )
    return (output, filter_grad)


def solution(mesh):
    return jax.shard_map(
        body,
        mesh=mesh,
        in_specs=(
            P("ctx", "ch"),
            P("ctx", "ch"),
            P("ctx", "ch"),
            P("ch"),
            P("ch", None),
            P("ctx", "ch"),
        ),
        out_specs=(P("ctx", "ch"), P("ctx", "ch")),
        check_vma=False,
    )
```

```python
import functools
import math

import jax
import jax.numpy as jnp
from jax import lax
from jax.experimental import pallas as pl
from jax.experimental.pallas import tpu as pltpu
from jax.sharding import PartitionSpec as P

exact_prec = lax.Precision.HIGHEST


def spectral_tables(block_len):
    time_ids = jnp.arange(2 * block_len, dtype=jnp.int32)
    freq_ids = jnp.arange(block_len, dtype=jnp.int32)
    phase_ids = freq_ids[:, None] * time_ids[None, :] % (2 * block_len)
    angles = phase_ids.astype(jnp.float32) * (math.pi / block_len)
    parity = jnp.where(time_ids % 2 == 0, 1.0, -1.0).astype(jnp.float32)[None, :]
    is_first = (freq_ids == 0)[:, None]
    forward = jnp.concatenate(
        [jnp.cos(angles), jnp.where(is_first, parity, -jnp.sin(angles))], axis=0
    )
    norm_scale = 1.0 / (2 * block_len)
    real_rows = jnp.where(is_first, 1.0, 2.0) * jnp.cos(angles) * norm_scale
    imag_rows = jnp.where(is_first, parity, -2.0 * jnp.sin(angles)) * norm_scale
    inverse = jnp.concatenate([real_rows, imag_rows], axis=0).T
    first_bin = is_first.astype(jnp.float32)
    return (forward, inverse, first_bin)


def spec_product(first_spec, second_spec, first_bin):
    bin_count = first_bin.shape[0]
    first_real, first_imag = (first_spec[..., :bin_count, :], first_spec[..., bin_count:, :])
    second_real, second_imag = (second_spec[..., :bin_count, :], second_spec[..., bin_count:, :])
    others = 1.0 - first_bin
    real_part = first_real * second_real - others * first_imag * second_imag
    imag_part = (
        others * (first_real * second_imag + first_imag * second_real)
        + first_bin * first_imag * second_imag
    )
    return jnp.concatenate([real_part, imag_part], axis=-2)


def conj_product(first_spec, second_spec, first_bin):
    bin_count = first_bin.shape[0]
    first_real, first_imag = (first_spec[..., :bin_count, :], first_spec[..., bin_count:, :])
    second_real, second_imag = (second_spec[..., :bin_count, :], second_spec[..., bin_count:, :])
    others = 1.0 - first_bin
    real_part = first_real * second_real + others * first_imag * second_imag
    imag_part = (
        others * (first_imag * second_real - first_real * second_imag)
        + first_bin * first_imag * second_imag
    )
    return jnp.concatenate([real_part, imag_part], axis=-2)


def transform(dft_table, block_rows):
    return jnp.dot(dft_table, block_rows.astype(jnp.float32), precision=exact_prec)


def shift_blocks(spec, blocks, width):
    if blocks == 0:
        return spec
    rows = spec.shape[0]
    pad = jnp.zeros((rows, blocks * width), spec.dtype)
    return jnp.concatenate([pad, spec[:, : spec.shape[1] - blocks * width]], axis=1)


def conv_products_kernel(width, low_ref, high_ref, taps_ref, conv_ref, seg_ref):
    rows, bins = low_ref.shape
    blocks = rows // width
    half = bins // 2
    for p in range(blocks):
        here = pl.ds(p * width, width)
        if p == 0:
            seg_ref[here, :] = high_ref[here, :]
        else:
            seg_ref[here, :] = high_ref[here, :] + low_ref[pl.ds((p - 1) * width, width), :]
    lane_ids = lax.broadcasted_iota(jnp.int32, (width, half), 1)
    first_bin = lane_ids == 0
    zero = jnp.zeros((width, half), jnp.float32)
    for p in range(blocks):
        acc_re, acc_im = zero, zero
        for k in range(p + 1):
            a_re, a_im = block_parts(taps_ref, k, width)
            b_re, b_im = block_parts(seg_ref, p - k, width)
            both_im = a_im * b_im
            acc_re = acc_re + a_re * b_re - jnp.where(first_bin, 0.0, both_im)
            acc_im = acc_im + jnp.where(first_bin, both_im, a_re * b_im + a_im * b_re)
        conv_ref[pl.ds(p * width, width), :half] = acc_re
        conv_ref[pl.ds(p * width, width), half:] = acc_im


def lag_products_kernel(width, seg_ref, grad_ref, lag_ref):
    rows, bins = seg_ref.shape
    blocks = rows // width
    half = bins // 2
    lane_ids = lax.broadcasted_iota(jnp.int32, (width, half), 1)
    first_bin = lane_ids == 0
    zero = jnp.zeros((width, half), jnp.float32)
    for k in range(blocks):
        acc_re, acc_im = zero, zero
        for p in range(k, blocks):
            a_re, a_im = block_parts(grad_ref, p, width)
            b_re, b_im = block_parts(seg_ref, p - k, width)
            both_im = a_im * b_im
            acc_re = acc_re + a_re * b_re + jnp.where(first_bin, 0.0, both_im)
            acc_im = acc_im + jnp.where(first_bin, both_im, a_im * b_re - a_re * b_im)
        lag_ref[pl.ds(k * width, width), :half] = acc_re
        lag_ref[pl.ds(k * width, width), half:] = acc_im


def block_parts(ref, i, width):
    half = ref.shape[1] // 2
    rows_i = pl.ds(i * width, width)
    return ref[rows_i, :half], ref[rows_i, half:]


def conv_products(low_spec, high_spec, taps_spec, width):
    rows, bins = low_spec.shape
    blocks = rows // width
    vmem = pl.BlockSpec(memory_space=pltpu.VMEM)
    shape = jax.ShapeDtypeStruct(low_spec.shape, jnp.float32)
    return pl.pallas_call(
        functools.partial(conv_products_kernel, width),
        out_shape=(shape, shape),
        in_specs=[vmem, vmem, vmem],
        out_specs=(vmem, vmem),
        cost_estimate=pl.CostEstimate(
            flops=blocks * (blocks + 1) // 2 * width * bins * 4,
            bytes_accessed=5 * rows * bins * 4,
            transcendentals=0,
        ),
    )(low_spec, high_spec, taps_spec)


def lag_products(seg_spec, grad_spec, width):
    rows, bins = seg_spec.shape
    blocks = rows // width
    vmem = pl.BlockSpec(memory_space=pltpu.VMEM)
    return pl.pallas_call(
        functools.partial(lag_products_kernel, width),
        out_shape=jax.ShapeDtypeStruct(seg_spec.shape, jnp.float32),
        in_specs=[vmem, vmem],
        out_specs=vmem,
        cost_estimate=pl.CostEstimate(
            flops=blocks * (blocks + 1) // 2 * width * bins * 4,
            bytes_accessed=3 * rows * bins * 4,
            transcendentals=0,
        ),
    )(seg_spec, grad_spec)


def transform_t(dft_table, block_rows):
    return lax.dot_general(
        block_rows.astype(jnp.float32), dft_table, (((1,), (1,)), ((), ())),
        precision=exact_prec,
    )


def inverse_t(inverse_rows, spec_t):
    return lax.dot_general(
        spec_t, inverse_rows, (((1,), (1,)), ((), ())), precision=exact_prec
    )


def body(inputs, gating, filter_taps, skip_gain, w_out, cotangent):
    block_len, channels = inputs.shape
    ctx_count = lax.axis_size("ctx")
    width = channels // ctx_count
    forward, inverse, first_bin = spectral_tables(block_len)
    first_half = forward[:, :block_len]
    second_half = forward[:, block_len:]

    pair = jnp.stack([inputs.T, filter_taps.T])
    pair_t = lax.all_to_all(pair, "ctx", 1, 1, tiled=True)
    signal_t, taps_t = pair_t[0], pair_t[1]

    ch_count = lax.axis_size("ch")
    me_ch = lax.axis_index("ch")
    upstream = jnp.zeros((block_len, channels), jnp.float32)
    for shift in range(ch_count):
        if shift == 0:
            block = cotangent
        else:
            block = lax.ppermute(
                cotangent, "ch",
                perm=[(j, (j + shift) % ch_count) for j in range(ch_count)],
            )
        owner = (me_ch - shift + ch_count) % ch_count
        w_cols = lax.dynamic_slice_in_dim(w_out, owner * channels, channels, 1)
        upstream = upstream + lax.dot_general(
            block, w_cols, (((1,), (1,)), ((), ())),
            preferred_element_type=jnp.float32,
        )
    gate_wide = gating.astype(jnp.float32)
    grad_mixed = upstream * gate_wide

    conv_spec, seg_spec = conv_products(
        transform_t(first_half, signal_t),
        transform_t(second_half, signal_t),
        transform_t(first_half, taps_t),
        width,
    )

    convolved_t = inverse_t(inverse[block_len:], conv_spec)
    convolved = lax.all_to_all(
        convolved_t.astype(jnp.bfloat16), "ctx", 0, 0, tiled=True
    ).T.astype(jnp.float32)

    mixed_sum = convolved + skip_gain[None, :] * inputs.astype(jnp.float32)
    gated_rows = (gate_wide * mixed_sum).astype(jnp.bfloat16)
    partial_out = jnp.dot(gated_rows, w_out, preferred_element_type=jnp.float32)
    pieces = lax.all_to_all(partial_out.astype(jnp.bfloat16), "ch", 1, 0, tiled=True)
    pieces, grad_mixed = lax.optimization_barrier((pieces, grad_mixed))
    grad_t = lax.all_to_all(grad_mixed.T.astype(jnp.bfloat16), "ctx", 0, 0, tiled=True)

    lag_spec = lag_products(seg_spec, transform_t(second_half, grad_t), width)
    filter_grad_t = inverse_t(inverse[:block_len], lag_spec)
    filter_grad = lax.all_to_all(
        filter_grad_t.astype(jnp.bfloat16), "ctx", 0, 0, tiled=True
    ).T.astype(jnp.float32)

    output = (
        pieces.astype(jnp.float32)
        .reshape(ch_count, block_len, channels)
        .sum(axis=0)
        .astype(jnp.bfloat16)
    )
    return (output, filter_grad)


def solution(mesh):
    return jax.shard_map(
        body,
        mesh=mesh,
        in_specs=(
            P("ctx", "ch"),
            P("ctx", "ch"),
            P("ctx", "ch"),
            P("ch"),
            P("ch", None),
            P("ctx", "ch"),
        ),
        out_specs=(P("ctx", "ch"), P("ctx", "ch")),
        check_vma=False,
    )
```

```python
import functools
import math

import jax
import jax.numpy as jnp
from jax import lax
from jax.experimental import pallas as pl
from jax.experimental.pallas import tpu as pltpu
from jax.sharding import PartitionSpec as P

exact_prec = lax.Precision.HIGHEST


def spectral_tables(block_len):
    time_ids = jnp.arange(2 * block_len, dtype=jnp.int32)
    freq_ids = jnp.arange(block_len, dtype=jnp.int32)
    phase_ids = freq_ids[:, None] * time_ids[None, :] % (2 * block_len)
    angles = phase_ids.astype(jnp.float32) * (math.pi / block_len)
    parity = jnp.where(time_ids % 2 == 0, 1.0, -1.0).astype(jnp.float32)[None, :]
    is_first = (freq_ids == 0)[:, None]
    forward = jnp.concatenate(
        [jnp.cos(angles), jnp.where(is_first, parity, -jnp.sin(angles))], axis=0
    )
    norm_scale = 1.0 / (2 * block_len)
    real_rows = jnp.where(is_first, 1.0, 2.0) * jnp.cos(angles) * norm_scale
    imag_rows = jnp.where(is_first, parity, -2.0 * jnp.sin(angles)) * norm_scale
    inverse = jnp.concatenate([real_rows, imag_rows], axis=0).T
    first_bin = is_first.astype(jnp.float32)
    return (forward, inverse, first_bin)


def spec_product(first_spec, second_spec, first_bin):
    bin_count = first_bin.shape[0]
    first_real, first_imag = (first_spec[..., :bin_count, :], first_spec[..., bin_count:, :])
    second_real, second_imag = (second_spec[..., :bin_count, :], second_spec[..., bin_count:, :])
    others = 1.0 - first_bin
    real_part = first_real * second_real - others * first_imag * second_imag
    imag_part = (
        others * (first_real * second_imag + first_imag * second_real)
        + first_bin * first_imag * second_imag
    )
    return jnp.concatenate([real_part, imag_part], axis=-2)


def conj_product(first_spec, second_spec, first_bin):
    bin_count = first_bin.shape[0]
    first_real, first_imag = (first_spec[..., :bin_count, :], first_spec[..., bin_count:, :])
    second_real, second_imag = (second_spec[..., :bin_count, :], second_spec[..., bin_count:, :])
    others = 1.0 - first_bin
    real_part = first_real * second_real + others * first_imag * second_imag
    imag_part = (
        others * (first_imag * second_real - first_real * second_imag)
        + first_bin * first_imag * second_imag
    )
    return jnp.concatenate([real_part, imag_part], axis=-2)


def transform(dft_table, block_rows):
    return jnp.dot(dft_table, block_rows.astype(jnp.float32), precision=exact_prec)


def shift_blocks(spec, blocks, width):
    if blocks == 0:
        return spec
    rows = spec.shape[0]
    pad = jnp.zeros((rows, blocks * width), spec.dtype)
    return jnp.concatenate([pad, spec[:, : spec.shape[1] - blocks * width]], axis=1)


def conv_products_kernel(width, low_ref, high_ref, taps_ref, conv_ref, seg_ref):
    rows, bins = low_ref.shape
    blocks = rows // width
    half = bins // 2
    for p in range(blocks):
        here = pl.ds(p * width, width)
        if p == 0:
            seg_ref[here, :] = high_ref[here, :]
        else:
            seg_ref[here, :] = high_ref[here, :] + low_ref[pl.ds((p - 1) * width, width), :]
    lane_ids = lax.broadcasted_iota(jnp.int32, (width, half), 1)
    first_bin = lane_ids == 0
    zero = jnp.zeros((width, half), jnp.float32)
    for p in range(blocks):
        acc_re, acc_im = zero, zero
        for k in range(p + 1):
            a_re, a_im = block_parts(taps_ref, k, width)
            b_re, b_im = block_parts(seg_ref, p - k, width)
            both_im = a_im * b_im
            acc_re = acc_re + a_re * b_re - jnp.where(first_bin, 0.0, both_im)
            acc_im = acc_im + jnp.where(first_bin, both_im, a_re * b_im + a_im * b_re)
        conv_ref[pl.ds(p * width, width), :half] = acc_re
        conv_ref[pl.ds(p * width, width), half:] = acc_im


def lag_products_kernel(width, seg_ref, grad_ref, lag_ref):
    rows, bins = seg_ref.shape
    blocks = rows // width
    half = bins // 2
    lane_ids = lax.broadcasted_iota(jnp.int32, (width, half), 1)
    first_bin = lane_ids == 0
    zero = jnp.zeros((width, half), jnp.float32)
    for k in range(blocks):
        acc_re, acc_im = zero, zero
        for p in range(k, blocks):
            a_re, a_im = block_parts(grad_ref, p, width)
            b_re, b_im = block_parts(seg_ref, p - k, width)
            both_im = a_im * b_im
            acc_re = acc_re + a_re * b_re + jnp.where(first_bin, 0.0, both_im)
            acc_im = acc_im + jnp.where(first_bin, both_im, a_im * b_re - a_re * b_im)
        lag_ref[pl.ds(k * width, width), :half] = acc_re
        lag_ref[pl.ds(k * width, width), half:] = acc_im


def block_parts(ref, i, width):
    half = ref.shape[1] // 2
    rows_i = pl.ds(i * width, width)
    return ref[rows_i, :half], ref[rows_i, half:]


def conv_products(low_spec, high_spec, taps_spec, width):
    rows, bins = low_spec.shape
    blocks = rows // width
    vmem = pl.BlockSpec(memory_space=pltpu.VMEM)
    shape = jax.ShapeDtypeStruct(low_spec.shape, jnp.float32)
    return pl.pallas_call(
        functools.partial(conv_products_kernel, width),
        out_shape=(shape, shape),
        in_specs=[vmem, vmem, vmem],
        out_specs=(vmem, vmem),
        cost_estimate=pl.CostEstimate(
            flops=blocks * (blocks + 1) // 2 * width * bins * 4,
            bytes_accessed=5 * rows * bins * 4,
            transcendentals=0,
        ),
    )(low_spec, high_spec, taps_spec)


def lag_products(seg_spec, grad_spec, width):
    rows, bins = seg_spec.shape
    blocks = rows // width
    vmem = pl.BlockSpec(memory_space=pltpu.VMEM)
    return pl.pallas_call(
        functools.partial(lag_products_kernel, width),
        out_shape=jax.ShapeDtypeStruct(seg_spec.shape, jnp.float32),
        in_specs=[vmem, vmem],
        out_specs=vmem,
        cost_estimate=pl.CostEstimate(
            flops=blocks * (blocks + 1) // 2 * width * bins * 4,
            bytes_accessed=3 * rows * bins * 4,
            transcendentals=0,
        ),
    )(seg_spec, grad_spec)


def transform_t(dft_table, block_rows):
    return lax.dot_general(
        block_rows.astype(jnp.float32), dft_table, (((1,), (1,)), ((), ())),
        precision=exact_prec,
    )


def inverse_t(inverse_rows, spec_t):
    return lax.dot_general(
        spec_t, inverse_rows, (((1,), (1,)), ((), ())), precision=exact_prec
    )


def body(inputs, gating, filter_taps, skip_gain, w_out, cotangent):
    block_len, channels = inputs.shape
    ctx_count = lax.axis_size("ctx")
    width = channels // ctx_count
    forward, inverse, first_bin = spectral_tables(block_len)
    first_half = forward[:, :block_len]
    second_half = forward[:, block_len:]

    pair = jnp.stack([inputs.T, filter_taps.T])
    pair_t = lax.all_to_all(pair, "ctx", 1, 1, tiled=True)
    signal_t, taps_t = pair_t[0], pair_t[1]

    ch_count = lax.axis_size(("chy", "chx"))
    cot_rows = lax.all_gather(
        lax.all_gather(cotangent, "chx", axis=1, tiled=True), "chy", axis=1, tiled=True
    )
    upstream = lax.dot_general(
        cot_rows,
        w_out,
        (((1,), (1,)), ((), ())),
        preferred_element_type=jnp.float32,
    )
    gate_wide = gating.astype(jnp.float32)
    grad_mixed = upstream * gate_wide

    conv_spec, seg_spec = conv_products(
        transform_t(first_half, signal_t),
        transform_t(second_half, signal_t),
        transform_t(first_half, taps_t),
        width,
    )

    convolved_t = inverse_t(inverse[block_len:], conv_spec)
    convolved = lax.all_to_all(
        convolved_t.astype(jnp.bfloat16), "ctx", 0, 0, tiled=True
    ).T.astype(jnp.float32)

    mixed_sum = convolved + skip_gain[None, :] * inputs.astype(jnp.float32)
    gated_rows = (gate_wide * mixed_sum).astype(jnp.bfloat16)
    partial_out = jnp.dot(gated_rows, w_out, preferred_element_type=jnp.float32)
    pieces = lax.all_to_all(partial_out.astype(jnp.bfloat16), ("chy", "chx"), 1, 0, tiled=True)
    pieces, grad_mixed = lax.optimization_barrier((pieces, grad_mixed))
    grad_t = lax.all_to_all(grad_mixed.T.astype(jnp.bfloat16), "ctx", 0, 0, tiled=True)

    lag_spec = lag_products(seg_spec, transform_t(second_half, grad_t), width)
    filter_grad_t = inverse_t(inverse[:block_len], lag_spec)
    filter_grad = lax.all_to_all(
        filter_grad_t.astype(jnp.bfloat16), "ctx", 0, 0, tiled=True
    ).T.astype(jnp.float32)

    output = (
        pieces.astype(jnp.float32)
        .reshape(ch_count, block_len, channels)
        .sum(axis=0)
        .astype(jnp.bfloat16)
    )
    return (output, filter_grad)


def solution(mesh):
    ch_y = mesh.shape["ch"] // 4
    split_mesh = jax.sharding.Mesh(
        mesh.devices.reshape(mesh.shape["ctx"], ch_y, 4), ("ctx", "chy", "chx")
    )
    ch = ("chy", "chx")
    return jax.shard_map(
        body,
        mesh=split_mesh,
        in_specs=(
            P("ctx", ch),
            P("ctx", ch),
            P("ctx", ch),
            P(ch),
            P(ch, None),
            P("ctx", ch),
        ),
        out_specs=(P("ctx", ch), P("ctx", ch)),
        check_vma=False,
    )
```

```python
import functools
import math

import jax
import jax.numpy as jnp
from jax import lax
from jax.experimental import pallas as pl
from jax.experimental.pallas import tpu as pltpu
from jax.sharding import PartitionSpec as P

exact_prec = lax.Precision.HIGHEST


def spectral_tables(block_len):
    time_ids = jnp.arange(2 * block_len, dtype=jnp.int32)
    freq_ids = jnp.arange(block_len, dtype=jnp.int32)
    phase_ids = freq_ids[:, None] * time_ids[None, :] % (2 * block_len)
    angles = phase_ids.astype(jnp.float32) * (math.pi / block_len)
    parity = jnp.where(time_ids % 2 == 0, 1.0, -1.0).astype(jnp.float32)[None, :]
    is_first = (freq_ids == 0)[:, None]
    forward = jnp.concatenate(
        [jnp.cos(angles), jnp.where(is_first, parity, -jnp.sin(angles))], axis=0
    )
    norm_scale = 1.0 / (2 * block_len)
    real_rows = jnp.where(is_first, 1.0, 2.0) * jnp.cos(angles) * norm_scale
    imag_rows = jnp.where(is_first, parity, -2.0 * jnp.sin(angles)) * norm_scale
    inverse = jnp.concatenate([real_rows, imag_rows], axis=0).T
    first_bin = is_first.astype(jnp.float32)
    return (forward, inverse, first_bin)


def spec_product(first_spec, second_spec, first_bin):
    bin_count = first_bin.shape[0]
    first_real, first_imag = (first_spec[..., :bin_count, :], first_spec[..., bin_count:, :])
    second_real, second_imag = (second_spec[..., :bin_count, :], second_spec[..., bin_count:, :])
    others = 1.0 - first_bin
    real_part = first_real * second_real - others * first_imag * second_imag
    imag_part = (
        others * (first_real * second_imag + first_imag * second_real)
        + first_bin * first_imag * second_imag
    )
    return jnp.concatenate([real_part, imag_part], axis=-2)


def conj_product(first_spec, second_spec, first_bin):
    bin_count = first_bin.shape[0]
    first_real, first_imag = (first_spec[..., :bin_count, :], first_spec[..., bin_count:, :])
    second_real, second_imag = (second_spec[..., :bin_count, :], second_spec[..., bin_count:, :])
    others = 1.0 - first_bin
    real_part = first_real * second_real + others * first_imag * second_imag
    imag_part = (
        others * (first_imag * second_real - first_real * second_imag)
        + first_bin * first_imag * second_imag
    )
    return jnp.concatenate([real_part, imag_part], axis=-2)


def transform(dft_table, block_rows):
    return jnp.dot(dft_table, block_rows.astype(jnp.float32), precision=exact_prec)


def shift_blocks(spec, blocks, width):
    if blocks == 0:
        return spec
    rows = spec.shape[0]
    pad = jnp.zeros((rows, blocks * width), spec.dtype)
    return jnp.concatenate([pad, spec[:, : spec.shape[1] - blocks * width]], axis=1)


def conv_products_kernel(width, low_ref, high_ref, taps_ref, conv_ref, seg_ref):
    rows, bins = low_ref.shape
    blocks = rows // width
    half = bins // 2
    for p in range(blocks):
        here = pl.ds(p * width, width)
        if p == 0:
            seg_ref[here, :] = high_ref[here, :]
        else:
            seg_ref[here, :] = high_ref[here, :] + low_ref[pl.ds((p - 1) * width, width), :]
    lane_ids = lax.broadcasted_iota(jnp.int32, (width, half), 1)
    first_bin = lane_ids == 0
    zero = jnp.zeros((width, half), jnp.float32)
    for p in range(blocks):
        acc_re, acc_im = zero, zero
        for k in range(p + 1):
            a_re, a_im = block_parts(taps_ref, k, width)
            b_re, b_im = block_parts(seg_ref, p - k, width)
            both_im = a_im * b_im
            acc_re = acc_re + a_re * b_re - jnp.where(first_bin, 0.0, both_im)
            acc_im = acc_im + jnp.where(first_bin, both_im, a_re * b_im + a_im * b_re)
        conv_ref[pl.ds(p * width, width), :half] = acc_re
        conv_ref[pl.ds(p * width, width), half:] = acc_im


def lag_products_kernel(width, seg_ref, grad_ref, lag_ref):
    rows, bins = seg_ref.shape
    blocks = rows // width
    half = bins // 2
    lane_ids = lax.broadcasted_iota(jnp.int32, (width, half), 1)
    first_bin = lane_ids == 0
    zero = jnp.zeros((width, half), jnp.float32)
    for k in range(blocks):
        acc_re, acc_im = zero, zero
        for p in range(k, blocks):
            a_re, a_im = block_parts(grad_ref, p, width)
            b_re, b_im = block_parts(seg_ref, p - k, width)
            both_im = a_im * b_im
            acc_re = acc_re + a_re * b_re + jnp.where(first_bin, 0.0, both_im)
            acc_im = acc_im + jnp.where(first_bin, both_im, a_im * b_re - a_re * b_im)
        lag_ref[pl.ds(k * width, width), :half] = acc_re
        lag_ref[pl.ds(k * width, width), half:] = acc_im


def block_parts(ref, i, width):
    half = ref.shape[1] // 2
    rows_i = pl.ds(i * width, width)
    return ref[rows_i, :half], ref[rows_i, half:]


def conv_products(low_spec, high_spec, taps_spec, width):
    rows, bins = low_spec.shape
    blocks = rows // width
    vmem = pl.BlockSpec(memory_space=pltpu.VMEM)
    shape = jax.ShapeDtypeStruct(low_spec.shape, jnp.float32)
    return pl.pallas_call(
        functools.partial(conv_products_kernel, width),
        out_shape=(shape, shape),
        in_specs=[vmem, vmem, vmem],
        out_specs=(vmem, vmem),
        cost_estimate=pl.CostEstimate(
            flops=blocks * (blocks + 1) // 2 * width * bins * 4,
            bytes_accessed=5 * rows * bins * 4,
            transcendentals=0,
        ),
    )(low_spec, high_spec, taps_spec)


def lag_products(seg_spec, grad_spec, width):
    rows, bins = seg_spec.shape
    blocks = rows // width
    vmem = pl.BlockSpec(memory_space=pltpu.VMEM)
    return pl.pallas_call(
        functools.partial(lag_products_kernel, width),
        out_shape=jax.ShapeDtypeStruct(seg_spec.shape, jnp.float32),
        in_specs=[vmem, vmem],
        out_specs=vmem,
        cost_estimate=pl.CostEstimate(
            flops=blocks * (blocks + 1) // 2 * width * bins * 4,
            bytes_accessed=3 * rows * bins * 4,
            transcendentals=0,
        ),
    )(seg_spec, grad_spec)


def transform_t(dft_table, block_rows):
    return lax.dot_general(
        block_rows.astype(jnp.float32), dft_table, (((1,), (1,)), ((), ())),
        precision=exact_prec,
    )


def inverse_t(inverse_rows, spec_t):
    return lax.dot_general(
        spec_t, inverse_rows, (((1,), (1,)), ((), ())), precision=exact_prec
    )


def body(inputs, gating, filter_taps, skip_gain, w_out, cotangent):
    block_len, channels = inputs.shape
    ctx_count = lax.axis_size("ctx")
    width = channels // ctx_count
    forward, inverse, first_bin = spectral_tables(block_len)
    first_half = forward[:, :block_len]
    second_half = forward[:, block_len:]

    pair = jnp.concatenate([inputs.T, filter_taps.T], axis=1)
    pair_t = lax.all_to_all(pair, "ctx", 0, 0, tiled=True)
    signal_t, taps_t = pair_t[:, :block_len], pair_t[:, block_len:]

    ch_count = lax.axis_size("ch")
    cot_rows = lax.all_gather(cotangent, "ch", axis=1, tiled=True)
    upstream = lax.dot_general(
        cot_rows,
        w_out,
        (((1,), (1,)), ((), ())),
        preferred_element_type=jnp.float32,
    )
    gate_wide = gating.astype(jnp.float32)
    grad_mixed = upstream * gate_wide

    conv_spec, seg_spec = conv_products(
        transform_t(first_half, signal_t),
        transform_t(second_half, signal_t),
        transform_t(first_half, taps_t),
        width,
    )

    convolved_t = inverse_t(inverse[block_len:], conv_spec)
    convolved = lax.all_to_all(
        convolved_t.astype(jnp.bfloat16), "ctx", 0, 0, tiled=True
    ).T.astype(jnp.float32)

    mixed_sum = convolved + skip_gain[None, :] * inputs.astype(jnp.float32)
    gated_rows = (gate_wide * mixed_sum).astype(jnp.bfloat16)
    partial_out = jnp.dot(gated_rows, w_out, preferred_element_type=jnp.float32)
    pieces = lax.all_to_all(partial_out.astype(jnp.bfloat16), "ch", 1, 0, tiled=True)
    pieces, grad_mixed = lax.optimization_barrier((pieces, grad_mixed))
    grad_t = lax.all_to_all(grad_mixed.T.astype(jnp.bfloat16), "ctx", 0, 0, tiled=True)

    lag_spec = lag_products(seg_spec, transform_t(second_half, grad_t), width)
    filter_grad_t = inverse_t(inverse[:block_len], lag_spec)
    filter_grad = lax.all_to_all(
        filter_grad_t.astype(jnp.bfloat16), "ctx", 0, 0, tiled=True
    ).T.astype(jnp.float32)

    output = (
        pieces.astype(jnp.float32)
        .reshape(ch_count, block_len, channels)
        .sum(axis=0)
        .astype(jnp.bfloat16)
    )
    return (output, filter_grad)


def solution(mesh):
    return jax.shard_map(
        body,
        mesh=mesh,
        in_specs=(
            P("ctx", "ch"),
            P("ctx", "ch"),
            P("ctx", "ch"),
            P("ch"),
            P("ch", None),
            P("ctx", "ch"),
        ),
        out_specs=(P("ctx", "ch"), P("ctx", "ch")),
        check_vma=False,
    )
```

```python
import functools
import math

import jax
import jax.numpy as jnp
from jax import lax
from jax.experimental import pallas as pl
from jax.experimental.pallas import tpu as pltpu
from jax.sharding import PartitionSpec as P

exact_prec = lax.Precision.HIGH


def spectral_tables(block_len):
    time_ids = jnp.arange(2 * block_len, dtype=jnp.int32)
    freq_ids = jnp.arange(block_len, dtype=jnp.int32)
    phase_ids = freq_ids[:, None] * time_ids[None, :] % (2 * block_len)
    angles = phase_ids.astype(jnp.float32) * (math.pi / block_len)
    parity = jnp.where(time_ids % 2 == 0, 1.0, -1.0).astype(jnp.float32)[None, :]
    is_first = (freq_ids == 0)[:, None]
    forward = jnp.concatenate(
        [jnp.cos(angles), jnp.where(is_first, parity, -jnp.sin(angles))], axis=0
    )
    norm_scale = 1.0 / (2 * block_len)
    real_rows = jnp.where(is_first, 1.0, 2.0) * jnp.cos(angles) * norm_scale
    imag_rows = jnp.where(is_first, parity, -2.0 * jnp.sin(angles)) * norm_scale
    inverse = jnp.concatenate([real_rows, imag_rows], axis=0).T
    first_bin = is_first.astype(jnp.float32)
    return (forward, inverse, first_bin)


def spec_product(first_spec, second_spec, first_bin):
    bin_count = first_bin.shape[0]
    first_real, first_imag = (first_spec[..., :bin_count, :], first_spec[..., bin_count:, :])
    second_real, second_imag = (second_spec[..., :bin_count, :], second_spec[..., bin_count:, :])
    others = 1.0 - first_bin
    real_part = first_real * second_real - others * first_imag * second_imag
    imag_part = (
        others * (first_real * second_imag + first_imag * second_real)
        + first_bin * first_imag * second_imag
    )
    return jnp.concatenate([real_part, imag_part], axis=-2)


def conj_product(first_spec, second_spec, first_bin):
    bin_count = first_bin.shape[0]
    first_real, first_imag = (first_spec[..., :bin_count, :], first_spec[..., bin_count:, :])
    second_real, second_imag = (second_spec[..., :bin_count, :], second_spec[..., bin_count:, :])
    others = 1.0 - first_bin
    real_part = first_real * second_real + others * first_imag * second_imag
    imag_part = (
        others * (first_imag * second_real - first_real * second_imag)
        + first_bin * first_imag * second_imag
    )
    return jnp.concatenate([real_part, imag_part], axis=-2)


def transform(dft_table, block_rows):
    return jnp.dot(dft_table, block_rows.astype(jnp.float32), precision=exact_prec)


def shift_blocks(spec, blocks, width):
    if blocks == 0:
        return spec
    rows = spec.shape[0]
    pad = jnp.zeros((rows, blocks * width), spec.dtype)
    return jnp.concatenate([pad, spec[:, : spec.shape[1] - blocks * width]], axis=1)


def conv_products_kernel(width, low_ref, high_ref, taps_ref, conv_ref, seg_ref):
    rows, bins = low_ref.shape
    blocks = rows // width
    half = bins // 2
    for p in range(blocks):
        here = pl.ds(p * width, width)
        if p == 0:
            seg_ref[here, :] = high_ref[here, :]
        else:
            seg_ref[here, :] = high_ref[here, :] + low_ref[pl.ds((p - 1) * width, width), :]
    lane_ids = lax.broadcasted_iota(jnp.int32, (width, half), 1)
    first_bin = lane_ids == 0
    zero = jnp.zeros((width, half), jnp.float32)
    for p in range(blocks):
        acc_re, acc_im = zero, zero
        for k in range(p + 1):
            a_re, a_im = block_parts(taps_ref, k, width)
            b_re, b_im = block_parts(seg_ref, p - k, width)
            both_im = a_im * b_im
            acc_re = acc_re + a_re * b_re - jnp.where(first_bin, 0.0, both_im)
            acc_im = acc_im + jnp.where(first_bin, both_im, a_re * b_im + a_im * b_re)
        conv_ref[pl.ds(p * width, width), :half] = acc_re
        conv_ref[pl.ds(p * width, width), half:] = acc_im


def lag_products_kernel(width, seg_ref, grad_ref, lag_ref):
    rows, bins = seg_ref.shape
    blocks = rows // width
    half = bins // 2
    lane_ids = lax.broadcasted_iota(jnp.int32, (width, half), 1)
    first_bin = lane_ids == 0
    zero = jnp.zeros((width, half), jnp.float32)
    for k in range(blocks):
        acc_re, acc_im = zero, zero
        for p in range(k, blocks):
            a_re, a_im = block_parts(grad_ref, p, width)
            b_re, b_im = block_parts(seg_ref, p - k, width)
            both_im = a_im * b_im
            acc_re = acc_re + a_re * b_re + jnp.where(first_bin, 0.0, both_im)
            acc_im = acc_im + jnp.where(first_bin, both_im, a_im * b_re - a_re * b_im)
        lag_ref[pl.ds(k * width, width), :half] = acc_re
        lag_ref[pl.ds(k * width, width), half:] = acc_im


def block_parts(ref, i, width):
    half = ref.shape[1] // 2
    rows_i = pl.ds(i * width, width)
    return ref[rows_i, :half], ref[rows_i, half:]


def conv_products(low_spec, high_spec, taps_spec, width):
    rows, bins = low_spec.shape
    blocks = rows // width
    vmem = pl.BlockSpec(memory_space=pltpu.VMEM)
    shape = jax.ShapeDtypeStruct(low_spec.shape, jnp.float32)
    return pl.pallas_call(
        functools.partial(conv_products_kernel, width),
        out_shape=(shape, shape),
        in_specs=[vmem, vmem, vmem],
        out_specs=(vmem, vmem),
        cost_estimate=pl.CostEstimate(
            flops=blocks * (blocks + 1) // 2 * width * bins * 4,
            bytes_accessed=5 * rows * bins * 4,
            transcendentals=0,
        ),
    )(low_spec, high_spec, taps_spec)


def lag_products(seg_spec, grad_spec, width):
    rows, bins = seg_spec.shape
    blocks = rows // width
    vmem = pl.BlockSpec(memory_space=pltpu.VMEM)
    return pl.pallas_call(
        functools.partial(lag_products_kernel, width),
        out_shape=jax.ShapeDtypeStruct(seg_spec.shape, jnp.float32),
        in_specs=[vmem, vmem],
        out_specs=vmem,
        cost_estimate=pl.CostEstimate(
            flops=blocks * (blocks + 1) // 2 * width * bins * 4,
            bytes_accessed=3 * rows * bins * 4,
            transcendentals=0,
        ),
    )(seg_spec, grad_spec)


def transform_t(dft_table, block_rows):
    return lax.dot_general(
        block_rows.astype(jnp.float32), dft_table, (((1,), (1,)), ((), ())),
        precision=exact_prec,
    )


def inverse_t(inverse_rows, spec_t):
    return lax.dot_general(
        spec_t, inverse_rows, (((1,), (1,)), ((), ())), precision=exact_prec
    )


def body(inputs, gating, filter_taps, skip_gain, w_out, cotangent):
    block_len, channels = inputs.shape
    ctx_count = lax.axis_size("ctx")
    width = channels // ctx_count
    forward, inverse, first_bin = spectral_tables(block_len)
    first_half = forward[:, :block_len]
    second_half = forward[:, block_len:]

    pair = jnp.concatenate([inputs.T, filter_taps.T], axis=1)
    pair_t = lax.all_to_all(pair, "ctx", 0, 0, tiled=True)
    signal_t, taps_t = pair_t[:, :block_len], pair_t[:, block_len:]

    ch_count = lax.axis_size("ch")
    cot_rows = lax.all_gather(cotangent, "ch", axis=1, tiled=True)
    upstream = lax.dot_general(
        cot_rows,
        w_out,
        (((1,), (1,)), ((), ())),
        preferred_element_type=jnp.float32,
    )
    gate_wide = gating.astype(jnp.float32)
    grad_mixed = upstream * gate_wide

    conv_spec, seg_spec = conv_products(
        transform_t(first_half, signal_t),
        transform_t(second_half, signal_t),
        transform_t(first_half, taps_t),
        width,
    )

    convolved_t = inverse_t(inverse[block_len:], conv_spec)
    convolved = lax.all_to_all(
        convolved_t.astype(jnp.bfloat16), "ctx", 0, 0, tiled=True
    ).T.astype(jnp.float32)

    mixed_sum = convolved + skip_gain[None, :] * inputs.astype(jnp.float32)
    gated_rows = (gate_wide * mixed_sum).astype(jnp.bfloat16)
    partial_out = jnp.dot(gated_rows, w_out, preferred_element_type=jnp.float32)
    pieces = lax.all_to_all(partial_out.astype(jnp.bfloat16), "ch", 1, 0, tiled=True)
    pieces, grad_mixed = lax.optimization_barrier((pieces, grad_mixed))
    grad_t = lax.all_to_all(grad_mixed.T.astype(jnp.bfloat16), "ctx", 0, 0, tiled=True)

    lag_spec = lag_products(seg_spec, transform_t(second_half, grad_t), width)
    filter_grad_t = inverse_t(inverse[:block_len], lag_spec)
    filter_grad = lax.all_to_all(
        filter_grad_t.astype(jnp.bfloat16), "ctx", 0, 0, tiled=True
    ).T.astype(jnp.float32)

    output = (
        pieces.astype(jnp.float32)
        .reshape(ch_count, block_len, channels)
        .sum(axis=0)
        .astype(jnp.bfloat16)
    )
    return (output, filter_grad)


def solution(mesh):
    return jax.shard_map(
        body,
        mesh=mesh,
        in_specs=(
            P("ctx", "ch"),
            P("ctx", "ch"),
            P("ctx", "ch"),
            P("ch"),
            P("ch", None),
            P("ctx", "ch"),
        ),
        out_specs=(P("ctx", "ch"), P("ctx", "ch")),
        check_vma=False,
    )
```

```python
import functools
import math

import jax
import jax.numpy as jnp
from jax import lax
from jax.experimental import pallas as pl
from jax.experimental.pallas import tpu as pltpu
from jax.sharding import PartitionSpec as P

exact_prec = lax.Precision.HIGHEST


def spectral_tables(block_len):
    time_ids = jnp.arange(2 * block_len, dtype=jnp.int32)
    freq_ids = jnp.arange(block_len, dtype=jnp.int32)
    phase_ids = freq_ids[:, None] * time_ids[None, :] % (2 * block_len)
    angles = phase_ids.astype(jnp.float32) * (math.pi / block_len)
    parity = jnp.where(time_ids % 2 == 0, 1.0, -1.0).astype(jnp.float32)[None, :]
    is_first = (freq_ids == 0)[:, None]
    forward = jnp.concatenate(
        [jnp.cos(angles), jnp.where(is_first, parity, -jnp.sin(angles))], axis=0
    )
    norm_scale = 1.0 / (2 * block_len)
    real_rows = jnp.where(is_first, 1.0, 2.0) * jnp.cos(angles) * norm_scale
    imag_rows = jnp.where(is_first, parity, -2.0 * jnp.sin(angles)) * norm_scale
    inverse = jnp.concatenate([real_rows, imag_rows], axis=0).T
    first_bin = is_first.astype(jnp.float32)
    return (forward, inverse, first_bin)


def spec_product(first_spec, second_spec, first_bin):
    bin_count = first_bin.shape[0]
    first_real, first_imag = (first_spec[..., :bin_count, :], first_spec[..., bin_count:, :])
    second_real, second_imag = (second_spec[..., :bin_count, :], second_spec[..., bin_count:, :])
    others = 1.0 - first_bin
    real_part = first_real * second_real - others * first_imag * second_imag
    imag_part = (
        others * (first_real * second_imag + first_imag * second_real)
        + first_bin * first_imag * second_imag
    )
    return jnp.concatenate([real_part, imag_part], axis=-2)


def conj_product(first_spec, second_spec, first_bin):
    bin_count = first_bin.shape[0]
    first_real, first_imag = (first_spec[..., :bin_count, :], first_spec[..., bin_count:, :])
    second_real, second_imag = (second_spec[..., :bin_count, :], second_spec[..., bin_count:, :])
    others = 1.0 - first_bin
    real_part = first_real * second_real + others * first_imag * second_imag
    imag_part = (
        others * (first_imag * second_real - first_real * second_imag)
        + first_bin * first_imag * second_imag
    )
    return jnp.concatenate([real_part, imag_part], axis=-2)


def transform(dft_table, block_rows):
    return jnp.dot(dft_table, block_rows.astype(jnp.float32), precision=exact_prec)


def shift_blocks(spec, blocks, width):
    if blocks == 0:
        return spec
    rows = spec.shape[0]
    pad = jnp.zeros((rows, blocks * width), spec.dtype)
    return jnp.concatenate([pad, spec[:, : spec.shape[1] - blocks * width]], axis=1)


def conv_products_kernel(width, low_ref, high_ref, taps_ref, conv_ref, seg_ref):
    rows, bins = low_ref.shape
    blocks = rows // width
    half = bins // 2
    for p in range(blocks):
        here = pl.ds(p * width, width)
        if p == 0:
            seg_ref[here, :] = high_ref[here, :]
        else:
            seg_ref[here, :] = high_ref[here, :] + low_ref[pl.ds((p - 1) * width, width), :]
    lane_ids = lax.broadcasted_iota(jnp.int32, (width, half), 1)
    first_bin = lane_ids == 0
    zero = jnp.zeros((width, half), jnp.float32)
    for p in range(blocks):
        acc_re, acc_im = zero, zero
        for k in range(p + 1):
            a_re, a_im = block_parts(taps_ref, k, width)
            b_re, b_im = block_parts(seg_ref, p - k, width)
            both_im = a_im * b_im
            acc_re = acc_re + a_re * b_re - jnp.where(first_bin, 0.0, both_im)
            acc_im = acc_im + jnp.where(first_bin, both_im, a_re * b_im + a_im * b_re)
        conv_ref[pl.ds(p * width, width), :half] = acc_re
        conv_ref[pl.ds(p * width, width), half:] = acc_im


def lag_products_kernel(width, seg_ref, grad_ref, lag_ref):
    rows, bins = seg_ref.shape
    blocks = rows // width
    half = bins // 2
    lane_ids = lax.broadcasted_iota(jnp.int32, (width, half), 1)
    first_bin = lane_ids == 0
    zero = jnp.zeros((width, half), jnp.float32)
    for k in range(blocks):
        acc_re, acc_im = zero, zero
        for p in range(k, blocks):
            a_re, a_im = block_parts(grad_ref, p, width)
            b_re, b_im = block_parts(seg_ref, p - k, width)
            both_im = a_im * b_im
            acc_re = acc_re + a_re * b_re + jnp.where(first_bin, 0.0, both_im)
            acc_im = acc_im + jnp.where(first_bin, both_im, a_im * b_re - a_re * b_im)
        lag_ref[pl.ds(k * width, width), :half] = acc_re
        lag_ref[pl.ds(k * width, width), half:] = acc_im


def block_parts(ref, i, width):
    half = ref.shape[1] // 2
    rows_i = pl.ds(i * width, width)
    return ref[rows_i, :half], ref[rows_i, half:]


def conv_products(low_spec, high_spec, taps_spec, width):
    rows, bins = low_spec.shape
    blocks = rows // width
    vmem = pl.BlockSpec(memory_space=pltpu.VMEM)
    shape = jax.ShapeDtypeStruct(low_spec.shape, jnp.float32)
    return pl.pallas_call(
        functools.partial(conv_products_kernel, width),
        out_shape=(shape, shape),
        in_specs=[vmem, vmem, vmem],
        out_specs=(vmem, vmem),
        cost_estimate=pl.CostEstimate(
            flops=blocks * (blocks + 1) // 2 * width * bins * 4,
            bytes_accessed=5 * rows * bins * 4,
            transcendentals=0,
        ),
    )(low_spec, high_spec, taps_spec)


def lag_products(seg_spec, grad_spec, width):
    rows, bins = seg_spec.shape
    blocks = rows // width
    vmem = pl.BlockSpec(memory_space=pltpu.VMEM)
    return pl.pallas_call(
        functools.partial(lag_products_kernel, width),
        out_shape=jax.ShapeDtypeStruct(seg_spec.shape, jnp.float32),
        in_specs=[vmem, vmem],
        out_specs=vmem,
        cost_estimate=pl.CostEstimate(
            flops=blocks * (blocks + 1) // 2 * width * bins * 4,
            bytes_accessed=3 * rows * bins * 4,
            transcendentals=0,
        ),
    )(seg_spec, grad_spec)


def transform_t(dft_table, block_rows):
    return lax.dot_general(
        block_rows.astype(jnp.float32), dft_table, (((1,), (1,)), ((), ())),
        precision=exact_prec,
    )


def inverse_t(inverse_rows, spec_t):
    return lax.dot_general(
        spec_t, inverse_rows, (((1,), (1,)), ((), ())), precision=exact_prec
    )


def body(inputs, gating, filter_taps, skip_gain, w_out, cotangent):
    block_len, channels = inputs.shape
    ctx_count = lax.axis_size("ctx")
    width = channels // ctx_count
    forward, inverse, first_bin = spectral_tables(block_len)
    first_half = forward[:, :block_len]
    second_half = forward[:, block_len:]

    pair = jnp.concatenate([inputs.T, filter_taps.T], axis=1)
    pair_t = lax.all_to_all(pair, "ctx", 0, 0, tiled=True)
    signal_t, taps_t = pair_t[:, :block_len], pair_t[:, block_len:]

    ch_count = lax.axis_size("ch")
    cot_rows = lax.all_gather(cotangent, "ch", axis=1, tiled=True)
    upstream = lax.dot_general(
        cot_rows,
        w_out,
        (((1,), (1,)), ((), ())),
        preferred_element_type=jnp.float32,
    )
    gate_wide = gating.astype(jnp.float32)
    grad_mixed = upstream * gate_wide

    conv_spec, seg_spec = conv_products(
        transform_t(first_half, signal_t),
        transform_t(second_half, signal_t),
        transform_t(first_half, taps_t),
        width,
    )

    convolved_t = inverse_t(inverse[block_len:], conv_spec)
    convolved = lax.all_to_all(
        convolved_t.astype(jnp.bfloat16), "ctx", 0, 0, tiled=True
    ).T.astype(jnp.float32)

    mixed_sum = convolved + skip_gain[None, :] * inputs.astype(jnp.float32)
    gated_rows = (gate_wide * mixed_sum).astype(jnp.bfloat16)
    partial_out = jnp.dot(gated_rows, w_out, preferred_element_type=jnp.float32)
    pieces = lax.all_to_all(partial_out.astype(jnp.bfloat16), "ch", 1, 0, tiled=True)
    grad_t = lax.all_to_all(grad_mixed.T.astype(jnp.bfloat16), "ctx", 0, 0, tiled=True)

    lag_spec = lag_products(seg_spec, transform_t(second_half, grad_t), width)
    filter_grad_t = inverse_t(inverse[:block_len], lag_spec)
    filter_grad = lax.all_to_all(
        filter_grad_t.astype(jnp.bfloat16), "ctx", 0, 0, tiled=True
    ).T.astype(jnp.float32)

    output = (
        pieces.astype(jnp.float32)
        .reshape(ch_count, block_len, channels)
        .sum(axis=0)
        .astype(jnp.bfloat16)
    )
    return (output, filter_grad)


def solution(mesh):
    return jax.shard_map(
        body,
        mesh=mesh,
        in_specs=(
            P("ctx", "ch"),
            P("ctx", "ch"),
            P("ctx", "ch"),
            P("ch"),
            P("ch", None),
            P("ctx", "ch"),
        ),
        out_specs=(P("ctx", "ch"), P("ctx", "ch")),
        check_vma=False,
    )
```

```python
import functools
import math

import jax
import jax.numpy as jnp
from jax import lax
from jax.experimental import pallas as pl
from jax.experimental.pallas import tpu as pltpu
from jax.sharding import PartitionSpec as P

exact_prec = lax.Precision.HIGHEST


def spectral_tables(block_len):
    time_ids = jnp.arange(2 * block_len, dtype=jnp.int32)
    freq_ids = jnp.arange(block_len, dtype=jnp.int32)
    phase_ids = freq_ids[:, None] * time_ids[None, :] % (2 * block_len)
    angles = phase_ids.astype(jnp.float32) * (math.pi / block_len)
    parity = jnp.where(time_ids % 2 == 0, 1.0, -1.0).astype(jnp.float32)[None, :]
    is_first = (freq_ids == 0)[:, None]
    forward = jnp.concatenate(
        [jnp.cos(angles), jnp.where(is_first, parity, -jnp.sin(angles))], axis=0
    )
    norm_scale = 1.0 / (2 * block_len)
    real_rows = jnp.where(is_first, 1.0, 2.0) * jnp.cos(angles) * norm_scale
    imag_rows = jnp.where(is_first, parity, -2.0 * jnp.sin(angles)) * norm_scale
    inverse = jnp.concatenate([real_rows, imag_rows], axis=0).T
    first_bin = is_first.astype(jnp.float32)
    return (forward, inverse, first_bin)


def spec_product(first_spec, second_spec, first_bin):
    bin_count = first_bin.shape[0]
    first_real, first_imag = (first_spec[..., :bin_count, :], first_spec[..., bin_count:, :])
    second_real, second_imag = (second_spec[..., :bin_count, :], second_spec[..., bin_count:, :])
    others = 1.0 - first_bin
    real_part = first_real * second_real - others * first_imag * second_imag
    imag_part = (
        others * (first_real * second_imag + first_imag * second_real)
        + first_bin * first_imag * second_imag
    )
    return jnp.concatenate([real_part, imag_part], axis=-2)


def conj_product(first_spec, second_spec, first_bin):
    bin_count = first_bin.shape[0]
    first_real, first_imag = (first_spec[..., :bin_count, :], first_spec[..., bin_count:, :])
    second_real, second_imag = (second_spec[..., :bin_count, :], second_spec[..., bin_count:, :])
    others = 1.0 - first_bin
    real_part = first_real * second_real + others * first_imag * second_imag
    imag_part = (
        others * (first_imag * second_real - first_real * second_imag)
        + first_bin * first_imag * second_imag
    )
    return jnp.concatenate([real_part, imag_part], axis=-2)


def transform(dft_table, block_rows):
    return jnp.dot(dft_table, block_rows.astype(jnp.float32), precision=exact_prec)


def shift_blocks(spec, blocks, width):
    if blocks == 0:
        return spec
    rows = spec.shape[0]
    pad = jnp.zeros((rows, blocks * width), spec.dtype)
    return jnp.concatenate([pad, spec[:, : spec.shape[1] - blocks * width]], axis=1)


def conv_products_kernel(width, low_ref, high_ref, taps_ref, conv_ref, seg_ref):
    rows, bins = low_ref.shape
    blocks = rows // width
    half = bins // 2
    for p in range(blocks):
        here = pl.ds(p * width, width)
        if p == 0:
            seg_ref[here, :] = high_ref[here, :]
        else:
            seg_ref[here, :] = high_ref[here, :] + low_ref[pl.ds((p - 1) * width, width), :]
    lane_ids = lax.broadcasted_iota(jnp.int32, (width, half), 1)
    first_bin = lane_ids == 0
    zero = jnp.zeros((width, half), jnp.float32)
    for p in range(blocks):
        acc_re, acc_im = zero, zero
        for k in range(p + 1):
            a_re, a_im = block_parts(taps_ref, k, width)
            b_re, b_im = block_parts(seg_ref, p - k, width)
            both_im = a_im * b_im
            acc_re = acc_re + a_re * b_re - jnp.where(first_bin, 0.0, both_im)
            acc_im = acc_im + jnp.where(first_bin, both_im, a_re * b_im + a_im * b_re)
        conv_ref[pl.ds(p * width, width), :half] = acc_re
        conv_ref[pl.ds(p * width, width), half:] = acc_im


def lag_products_kernel(width, seg_ref, grad_ref, lag_ref):
    rows, bins = seg_ref.shape
    blocks = rows // width
    half = bins // 2
    lane_ids = lax.broadcasted_iota(jnp.int32, (width, half), 1)
    first_bin = lane_ids == 0
    zero = jnp.zeros((width, half), jnp.float32)
    for k in range(blocks):
        acc_re, acc_im = zero, zero
        for p in range(k, blocks):
            a_re, a_im = block_parts(grad_ref, p, width)
            b_re, b_im = block_parts(seg_ref, p - k, width)
            both_im = a_im * b_im
            acc_re = acc_re + a_re * b_re + jnp.where(first_bin, 0.0, both_im)
            acc_im = acc_im + jnp.where(first_bin, both_im, a_im * b_re - a_re * b_im)
        lag_ref[pl.ds(k * width, width), :half] = acc_re
        lag_ref[pl.ds(k * width, width), half:] = acc_im


def block_parts(ref, i, width):
    half = ref.shape[1] // 2
    rows_i = pl.ds(i * width, width)
    return ref[rows_i, :half], ref[rows_i, half:]


def conv_products(low_spec, high_spec, taps_spec, width):
    rows, bins = low_spec.shape
    blocks = rows // width
    vmem = pl.BlockSpec(memory_space=pltpu.VMEM)
    shape = jax.ShapeDtypeStruct(low_spec.shape, jnp.float32)
    return pl.pallas_call(
        functools.partial(conv_products_kernel, width),
        out_shape=(shape, shape),
        in_specs=[vmem, vmem, vmem],
        out_specs=(vmem, vmem),
        cost_estimate=pl.CostEstimate(
            flops=blocks * (blocks + 1) // 2 * width * bins * 4,
            bytes_accessed=5 * rows * bins * 4,
            transcendentals=0,
        ),
    )(low_spec, high_spec, taps_spec)


def lag_products(seg_spec, grad_spec, width):
    rows, bins = seg_spec.shape
    blocks = rows // width
    vmem = pl.BlockSpec(memory_space=pltpu.VMEM)
    return pl.pallas_call(
        functools.partial(lag_products_kernel, width),
        out_shape=jax.ShapeDtypeStruct(seg_spec.shape, jnp.float32),
        in_specs=[vmem, vmem],
        out_specs=vmem,
        cost_estimate=pl.CostEstimate(
            flops=blocks * (blocks + 1) // 2 * width * bins * 4,
            bytes_accessed=3 * rows * bins * 4,
            transcendentals=0,
        ),
    )(seg_spec, grad_spec)


def transform_t(dft_table, block_rows):
    return lax.dot_general(
        block_rows.astype(jnp.float32), dft_table, (((1,), (1,)), ((), ())),
        precision=exact_prec,
    )


def inverse_t(inverse_rows, spec_t):
    return lax.dot_general(
        spec_t, inverse_rows, (((1,), (1,)), ((), ())), precision=exact_prec
    )


def body(inputs, gating, filter_taps, skip_gain, w_out, cotangent):
    block_len, channels = inputs.shape
    ctx_count = lax.axis_size("ctx")
    width = channels // ctx_count
    forward, inverse, first_bin = spectral_tables(block_len)
    first_half = forward[:, :block_len]
    second_half = forward[:, block_len:]

    pair = jnp.concatenate([inputs.T, filter_taps.T], axis=1)
    pair_t = lax.all_to_all(pair, "ctx", 0, 0, tiled=True)
    signal_t, taps_t = pair_t[:, :block_len], pair_t[:, block_len:]

    ch_count = lax.axis_size("ch")
    cot_rows = lax.all_gather(cotangent, "ch", axis=1, tiled=True)
    upstream = lax.dot_general(
        cot_rows,
        w_out,
        (((1,), (1,)), ((), ())),
        preferred_element_type=jnp.float32,
    )
    gate_wide = gating.astype(jnp.float32)
    grad_mixed = upstream * gate_wide

    conv_spec, seg_spec = conv_products(
        transform_t(first_half, signal_t),
        transform_t(second_half, signal_t),
        transform_t(first_half, taps_t),
        width,
    )

    convolved_t = inverse_t(inverse[block_len:], conv_spec)
    convolved = lax.all_to_all(
        convolved_t.astype(jnp.bfloat16), "ctx", 0, 0, tiled=True
    ).T.astype(jnp.float32)

    mixed_sum = convolved + skip_gain[None, :] * inputs.astype(jnp.float32)
    gated_rows = (gate_wide * mixed_sum).astype(jnp.bfloat16)
    partial_out = lax.dot_general(
        w_out, gated_rows, (((0,), (1,)), ((), ())), preferred_element_type=jnp.float32
    )
    pieces = lax.all_to_all(partial_out.astype(jnp.bfloat16), "ch", 0, 0, tiled=True)
    pieces, grad_mixed = lax.optimization_barrier((pieces, grad_mixed))
    grad_t = lax.all_to_all(grad_mixed.T.astype(jnp.bfloat16), "ctx", 0, 0, tiled=True)

    lag_spec = lag_products(seg_spec, transform_t(second_half, grad_t), width)
    filter_grad_t = inverse_t(inverse[:block_len], lag_spec)
    filter_grad = lax.all_to_all(
        filter_grad_t.astype(jnp.bfloat16), "ctx", 0, 0, tiled=True
    ).T.astype(jnp.float32)

    output = (
        pieces.astype(jnp.float32)
        .reshape(ch_count, channels, block_len)
        .sum(axis=0)
        .astype(jnp.bfloat16)
        .T
    )
    return (output, filter_grad)


def solution(mesh):
    return jax.shard_map(
        body,
        mesh=mesh,
        in_specs=(
            P("ctx", "ch"),
            P("ctx", "ch"),
            P("ctx", "ch"),
            P("ch"),
            P("ch", None),
            P("ctx", "ch"),
        ),
        out_specs=(P("ctx", "ch"), P("ctx", "ch")),
        check_vma=False,
    )
```

```python
import functools
import math

import jax
import jax.numpy as jnp
from jax import lax
from jax.experimental import pallas as pl
from jax.experimental.pallas import tpu as pltpu
from jax.sharding import PartitionSpec as P

exact_prec = lax.Precision.HIGHEST


def spectral_tables(block_len):
    time_ids = jnp.arange(2 * block_len, dtype=jnp.int32)
    freq_ids = jnp.arange(block_len, dtype=jnp.int32)
    phase_ids = freq_ids[:, None] * time_ids[None, :] % (2 * block_len)
    angles = phase_ids.astype(jnp.float32) * (math.pi / block_len)
    parity = jnp.where(time_ids % 2 == 0, 1.0, -1.0).astype(jnp.float32)[None, :]
    is_first = (freq_ids == 0)[:, None]
    forward = jnp.concatenate(
        [jnp.cos(angles), jnp.where(is_first, parity, -jnp.sin(angles))], axis=0
    )
    norm_scale = 1.0 / (2 * block_len)
    real_rows = jnp.where(is_first, 1.0, 2.0) * jnp.cos(angles) * norm_scale
    imag_rows = jnp.where(is_first, parity, -2.0 * jnp.sin(angles)) * norm_scale
    inverse = jnp.concatenate([real_rows, imag_rows], axis=0).T
    first_bin = is_first.astype(jnp.float32)
    return (forward, inverse, first_bin)


def spec_product(first_spec, second_spec, first_bin):
    bin_count = first_bin.shape[0]
    first_real, first_imag = (first_spec[..., :bin_count, :], first_spec[..., bin_count:, :])
    second_real, second_imag = (second_spec[..., :bin_count, :], second_spec[..., bin_count:, :])
    others = 1.0 - first_bin
    real_part = first_real * second_real - others * first_imag * second_imag
    imag_part = (
        others * (first_real * second_imag + first_imag * second_real)
        + first_bin * first_imag * second_imag
    )
    return jnp.concatenate([real_part, imag_part], axis=-2)


def conj_product(first_spec, second_spec, first_bin):
    bin_count = first_bin.shape[0]
    first_real, first_imag = (first_spec[..., :bin_count, :], first_spec[..., bin_count:, :])
    second_real, second_imag = (second_spec[..., :bin_count, :], second_spec[..., bin_count:, :])
    others = 1.0 - first_bin
    real_part = first_real * second_real + others * first_imag * second_imag
    imag_part = (
        others * (first_imag * second_real - first_real * second_imag)
        + first_bin * first_imag * second_imag
    )
    return jnp.concatenate([real_part, imag_part], axis=-2)


def transform(dft_table, block_rows):
    return jnp.dot(dft_table, block_rows.astype(jnp.float32), precision=exact_prec)


def shift_blocks(spec, blocks, width):
    if blocks == 0:
        return spec
    rows = spec.shape[0]
    pad = jnp.zeros((rows, blocks * width), spec.dtype)
    return jnp.concatenate([pad, spec[:, : spec.shape[1] - blocks * width]], axis=1)


def conv_products_kernel(width, low_ref, high_ref, taps_ref, conv_ref, seg_ref):
    rows, bins = low_ref.shape
    blocks = rows // width
    half = bins // 2
    for p in range(blocks):
        here = pl.ds(p * width, width)
        if p == 0:
            seg_ref[here, :] = high_ref[here, :]
        else:
            seg_ref[here, :] = high_ref[here, :] + low_ref[pl.ds((p - 1) * width, width), :]
    lane_ids = lax.broadcasted_iota(jnp.int32, (width, half), 1)
    first_bin = lane_ids == 0
    zero = jnp.zeros((width, half), jnp.float32)
    for p in range(blocks):
        acc_re, acc_im = zero, zero
        for k in range(p + 1):
            a_re, a_im = block_parts(taps_ref, k, width)
            b_re, b_im = block_parts(seg_ref, p - k, width)
            both_im = a_im * b_im
            acc_re = acc_re + a_re * b_re - jnp.where(first_bin, 0.0, both_im)
            acc_im = acc_im + jnp.where(first_bin, both_im, a_re * b_im + a_im * b_re)
        conv_ref[pl.ds(p * width, width), :half] = acc_re
        conv_ref[pl.ds(p * width, width), half:] = acc_im


def lag_products_kernel(width, seg_ref, grad_ref, lag_ref):
    rows, bins = seg_ref.shape
    blocks = rows // width
    half = bins // 2
    lane_ids = lax.broadcasted_iota(jnp.int32, (width, half), 1)
    first_bin = lane_ids == 0
    zero = jnp.zeros((width, half), jnp.float32)
    for k in range(blocks):
        acc_re, acc_im = zero, zero
        for p in range(k, blocks):
            a_re, a_im = block_parts(grad_ref, p, width)
            b_re, b_im = block_parts(seg_ref, p - k, width)
            both_im = a_im * b_im
            acc_re = acc_re + a_re * b_re + jnp.where(first_bin, 0.0, both_im)
            acc_im = acc_im + jnp.where(first_bin, both_im, a_im * b_re - a_re * b_im)
        lag_ref[pl.ds(k * width, width), :half] = acc_re
        lag_ref[pl.ds(k * width, width), half:] = acc_im


def block_parts(ref, i, width):
    half = ref.shape[1] // 2
    rows_i = pl.ds(i * width, width)
    return ref[rows_i, :half], ref[rows_i, half:]


def conv_products(low_spec, high_spec, taps_spec, width):
    rows, bins = low_spec.shape
    blocks = rows // width
    vmem = pl.BlockSpec(memory_space=pltpu.VMEM)
    shape = jax.ShapeDtypeStruct(low_spec.shape, jnp.float32)
    return pl.pallas_call(
        functools.partial(conv_products_kernel, width),
        out_shape=(shape, shape),
        in_specs=[vmem, vmem, vmem],
        out_specs=(vmem, vmem),
        cost_estimate=pl.CostEstimate(
            flops=blocks * (blocks + 1) // 2 * width * bins * 4,
            bytes_accessed=5 * rows * bins * 4,
            transcendentals=0,
        ),
    )(low_spec, high_spec, taps_spec)


def lag_products(seg_spec, grad_spec, width):
    rows, bins = seg_spec.shape
    blocks = rows // width
    vmem = pl.BlockSpec(memory_space=pltpu.VMEM)
    return pl.pallas_call(
        functools.partial(lag_products_kernel, width),
        out_shape=jax.ShapeDtypeStruct(seg_spec.shape, jnp.float32),
        in_specs=[vmem, vmem],
        out_specs=vmem,
        cost_estimate=pl.CostEstimate(
            flops=blocks * (blocks + 1) // 2 * width * bins * 4,
            bytes_accessed=3 * rows * bins * 4,
            transcendentals=0,
        ),
    )(seg_spec, grad_spec)


def transform_t(dft_table, block_rows):
    return lax.dot_general(
        block_rows.astype(jnp.float32), dft_table, (((1,), (1,)), ((), ())),
        precision=exact_prec,
    )


def inverse_t(inverse_rows, spec_t):
    return lax.dot_general(
        spec_t, inverse_rows, (((1,), (1,)), ((), ())), precision=exact_prec
    )


def body(inputs, gating, filter_taps, skip_gain, w_out, cotangent):
    block_len, channels = inputs.shape
    ctx_count = lax.axis_size("ctx")
    width = channels // ctx_count
    forward, inverse, first_bin = spectral_tables(block_len)
    first_half = forward[:, :block_len]
    second_half = forward[:, block_len:]

    pair = jnp.concatenate([inputs.T, filter_taps.T], axis=1)
    pair_t = lax.all_to_all(pair, "ctx", 0, 0, tiled=True)
    signal_t, taps_t = pair_t[:, :block_len], pair_t[:, block_len:]

    ch_count = lax.axis_size("ch")
    cot_rows = lax.all_gather(cotangent, "ch", axis=1, tiled=True)
    upstream_t = lax.dot_general(
        w_out,
        cot_rows,
        (((1,), (1,)), ((), ())),
        preferred_element_type=jnp.float32,
    )
    gate_wide = gating.astype(jnp.float32)
    grad_mixed_t = upstream_t * gate_wide.T

    conv_spec, seg_spec = conv_products(
        transform_t(first_half, signal_t),
        transform_t(second_half, signal_t),
        transform_t(first_half, taps_t),
        width,
    )

    convolved_t = inverse_t(inverse[block_len:], conv_spec)
    convolved = lax.all_to_all(
        convolved_t.astype(jnp.bfloat16), "ctx", 0, 0, tiled=True
    ).T.astype(jnp.float32)

    mixed_sum = convolved + skip_gain[None, :] * inputs.astype(jnp.float32)
    gated_rows = (gate_wide * mixed_sum).astype(jnp.bfloat16)
    partial_out = lax.dot_general(
        w_out, gated_rows, (((0,), (1,)), ((), ())), preferred_element_type=jnp.float32
    )
    pieces = lax.all_to_all(partial_out.astype(jnp.bfloat16), "ch", 0, 0, tiled=True)
    pieces, grad_mixed_t = lax.optimization_barrier((pieces, grad_mixed_t))
    grad_t = lax.all_to_all(grad_mixed_t.astype(jnp.bfloat16), "ctx", 0, 0, tiled=True)

    lag_spec = lag_products(seg_spec, transform_t(second_half, grad_t), width)
    filter_grad_t = inverse_t(inverse[:block_len], lag_spec)
    filter_grad = lax.all_to_all(
        filter_grad_t.astype(jnp.bfloat16), "ctx", 0, 0, tiled=True
    ).T.astype(jnp.float32)

    output = (
        pieces.astype(jnp.float32)
        .reshape(ch_count, channels, block_len)
        .sum(axis=0)
        .astype(jnp.bfloat16)
        .T
    )
    return (output, filter_grad)


def solution(mesh):
    return jax.shard_map(
        body,
        mesh=mesh,
        in_specs=(
            P("ctx", "ch"),
            P("ctx", "ch"),
            P("ctx", "ch"),
            P("ch"),
            P("ch", None),
            P("ctx", "ch"),
        ),
        out_specs=(P("ctx", "ch"), P("ctx", "ch")),
        check_vma=False,
    )
```

```python
import functools
import math

import jax
import jax.numpy as jnp
from jax import lax
from jax.experimental import pallas as pl
from jax.experimental.pallas import tpu as pltpu
from jax.sharding import PartitionSpec as P

exact_prec = lax.Precision.HIGHEST


def spectral_tables(block_len):
    time_ids = jnp.arange(2 * block_len, dtype=jnp.int32)
    freq_ids = jnp.arange(block_len, dtype=jnp.int32)
    phase_ids = freq_ids[:, None] * time_ids[None, :] % (2 * block_len)
    angles = phase_ids.astype(jnp.float32) * (math.pi / block_len)
    parity = jnp.where(time_ids % 2 == 0, 1.0, -1.0).astype(jnp.float32)[None, :]
    is_first = (freq_ids == 0)[:, None]
    forward = jnp.concatenate(
        [jnp.cos(angles), jnp.where(is_first, parity, -jnp.sin(angles))], axis=0
    )
    norm_scale = 1.0 / (2 * block_len)
    real_rows = jnp.where(is_first, 1.0, 2.0) * jnp.cos(angles) * norm_scale
    imag_rows = jnp.where(is_first, parity, -2.0 * jnp.sin(angles)) * norm_scale
    inverse = jnp.concatenate([real_rows, imag_rows], axis=0).T
    first_bin = is_first.astype(jnp.float32)
    return (forward, inverse, first_bin)


def spec_product(first_spec, second_spec, first_bin):
    bin_count = first_bin.shape[0]
    first_real, first_imag = (first_spec[..., :bin_count, :], first_spec[..., bin_count:, :])
    second_real, second_imag = (second_spec[..., :bin_count, :], second_spec[..., bin_count:, :])
    others = 1.0 - first_bin
    real_part = first_real * second_real - others * first_imag * second_imag
    imag_part = (
        others * (first_real * second_imag + first_imag * second_real)
        + first_bin * first_imag * second_imag
    )
    return jnp.concatenate([real_part, imag_part], axis=-2)


def conj_product(first_spec, second_spec, first_bin):
    bin_count = first_bin.shape[0]
    first_real, first_imag = (first_spec[..., :bin_count, :], first_spec[..., bin_count:, :])
    second_real, second_imag = (second_spec[..., :bin_count, :], second_spec[..., bin_count:, :])
    others = 1.0 - first_bin
    real_part = first_real * second_real + others * first_imag * second_imag
    imag_part = (
        others * (first_imag * second_real - first_real * second_imag)
        + first_bin * first_imag * second_imag
    )
    return jnp.concatenate([real_part, imag_part], axis=-2)


def transform(dft_table, block_rows):
    return jnp.dot(dft_table, block_rows.astype(jnp.float32), precision=exact_prec)


def shift_blocks(spec, blocks, width):
    if blocks == 0:
        return spec
    rows = spec.shape[0]
    pad = jnp.zeros((rows, blocks * width), spec.dtype)
    return jnp.concatenate([pad, spec[:, : spec.shape[1] - blocks * width]], axis=1)


def conv_products_kernel(width, low_ref, high_ref, taps_ref, conv_ref, seg_ref):
    rows, bins = low_ref.shape
    blocks = rows // width
    half = bins // 2
    for p in range(blocks):
        here = pl.ds(p * width, width)
        if p == 0:
            seg_ref[here, :] = high_ref[here, :]
        else:
            seg_ref[here, :] = high_ref[here, :] + low_ref[pl.ds((p - 1) * width, width), :]
    lane_ids = lax.broadcasted_iota(jnp.int32, (width, half), 1)
    first_bin = lane_ids == 0
    zero = jnp.zeros((width, half), jnp.float32)
    for p in range(blocks):
        acc_re, acc_im = zero, zero
        for k in range(p + 1):
            a_re, a_im = block_parts(taps_ref, k, width)
            b_re, b_im = block_parts(seg_ref, p - k, width)
            both_im = a_im * b_im
            acc_re = acc_re + a_re * b_re - jnp.where(first_bin, 0.0, both_im)
            acc_im = acc_im + jnp.where(first_bin, both_im, a_re * b_im + a_im * b_re)
        conv_ref[pl.ds(p * width, width), :half] = acc_re
        conv_ref[pl.ds(p * width, width), half:] = acc_im


def lag_products_kernel(width, seg_ref, grad_ref, lag_ref):
    rows, bins = seg_ref.shape
    blocks = rows // width
    half = bins // 2
    lane_ids = lax.broadcasted_iota(jnp.int32, (width, half), 1)
    first_bin = lane_ids == 0
    zero = jnp.zeros((width, half), jnp.float32)
    for k in range(blocks):
        acc_re, acc_im = zero, zero
        for p in range(k, blocks):
            a_re, a_im = block_parts(grad_ref, p, width)
            b_re, b_im = block_parts(seg_ref, p - k, width)
            both_im = a_im * b_im
            acc_re = acc_re + a_re * b_re + jnp.where(first_bin, 0.0, both_im)
            acc_im = acc_im + jnp.where(first_bin, both_im, a_im * b_re - a_re * b_im)
        lag_ref[pl.ds(k * width, width), :half] = acc_re
        lag_ref[pl.ds(k * width, width), half:] = acc_im


def block_parts(ref, i, width):
    half = ref.shape[1] // 2
    rows_i = pl.ds(i * width, width)
    return ref[rows_i, :half], ref[rows_i, half:]


def conv_products(low_spec, high_spec, taps_spec, width):
    rows, bins = low_spec.shape
    blocks = rows // width
    vmem = pl.BlockSpec(memory_space=pltpu.VMEM)
    shape = jax.ShapeDtypeStruct(low_spec.shape, jnp.float32)
    return pl.pallas_call(
        functools.partial(conv_products_kernel, width),
        out_shape=(shape, shape),
        in_specs=[vmem, vmem, vmem],
        out_specs=(vmem, vmem),
        cost_estimate=pl.CostEstimate(
            flops=blocks * (blocks + 1) // 2 * width * bins * 4,
            bytes_accessed=5 * rows * bins * 4,
            transcendentals=0,
        ),
    )(low_spec, high_spec, taps_spec)


def lag_products(seg_spec, grad_spec, width):
    rows, bins = seg_spec.shape
    blocks = rows // width
    vmem = pl.BlockSpec(memory_space=pltpu.VMEM)
    return pl.pallas_call(
        functools.partial(lag_products_kernel, width),
        out_shape=jax.ShapeDtypeStruct(seg_spec.shape, jnp.float32),
        in_specs=[vmem, vmem],
        out_specs=vmem,
        cost_estimate=pl.CostEstimate(
            flops=blocks * (blocks + 1) // 2 * width * bins * 4,
            bytes_accessed=3 * rows * bins * 4,
            transcendentals=0,
        ),
    )(seg_spec, grad_spec)


def transform_t(dft_table, block_rows):
    return lax.dot_general(
        block_rows.astype(jnp.float32), dft_table, (((1,), (1,)), ((), ())),
        precision=exact_prec,
    )


def inverse_t(inverse_rows, spec_t):
    return lax.dot_general(
        spec_t, inverse_rows, (((1,), (1,)), ((), ())), precision=exact_prec
    )


def body(inputs, gating, filter_taps, skip_gain, w_out, cotangent):
    block_len, channels = inputs.shape
    ctx_count = lax.axis_size("ctx")
    width = channels // ctx_count
    forward, inverse, first_bin = spectral_tables(block_len)
    first_half = forward[:, :block_len]
    second_half = forward[:, block_len:]

    pair = jnp.concatenate([inputs.T, filter_taps.T], axis=1)
    pair_t = lax.all_to_all(pair, "ctx", 0, 0, tiled=True)
    signal_t, taps_t = pair_t[:, :block_len], pair_t[:, block_len:]

    ch_count = lax.axis_size("ch")
    cot_rows = lax.all_gather(cotangent, "ch", axis=1, tiled=True)
    upstream_t = lax.dot_general(
        w_out,
        cot_rows,
        (((1,), (1,)), ((), ())),
        preferred_element_type=jnp.float32,
    )
    gate_wide = gating.astype(jnp.float32)
    grad_mixed_t = upstream_t * gate_wide.T

    conv_spec, seg_spec = conv_products(
        transform_t(first_half, signal_t),
        transform_t(second_half, signal_t),
        transform_t(first_half, taps_t),
        width,
    )

    convolved_t = inverse_t(inverse[block_len:], conv_spec)
    convolved_ct = lax.all_to_all(
        convolved_t.astype(jnp.bfloat16), "ctx", 0, 0, tiled=True
    ).astype(jnp.float32)

    mixed_ct = convolved_ct + skip_gain[:, None] * inputs.T.astype(jnp.float32)
    gated_ct = (gate_wide.T * mixed_ct).astype(jnp.bfloat16)
    partial_out = lax.dot_general(
        w_out, gated_ct, (((0,), (0,)), ((), ())), preferred_element_type=jnp.float32
    )
    pieces = lax.all_to_all(partial_out.astype(jnp.bfloat16), "ch", 0, 0, tiled=True)
    pieces, grad_mixed_t = lax.optimization_barrier((pieces, grad_mixed_t))
    grad_t = lax.all_to_all(grad_mixed_t.astype(jnp.bfloat16), "ctx", 0, 0, tiled=True)

    lag_spec = lag_products(seg_spec, transform_t(second_half, grad_t), width)
    filter_grad_t = inverse_t(inverse[:block_len], lag_spec)
    filter_grad = lax.all_to_all(
        filter_grad_t.astype(jnp.bfloat16), "ctx", 0, 0, tiled=True
    ).T.astype(jnp.float32)

    output = (
        pieces.astype(jnp.float32)
        .reshape(ch_count, channels, block_len)
        .sum(axis=0)
        .astype(jnp.bfloat16)
        .T
    )
    return (output, filter_grad)


def solution(mesh):
    return jax.shard_map(
        body,
        mesh=mesh,
        in_specs=(
            P("ctx", "ch"),
            P("ctx", "ch"),
            P("ctx", "ch"),
            P("ch"),
            P("ch", None),
            P("ctx", "ch"),
        ),
        out_specs=(P("ctx", "ch"), P("ctx", "ch")),
        check_vma=False,
    )
```
